512 devices in a mesh: grp: 16 (over z_hi, x, core), dev: 32 (over y, z_lo).
Axes of the slice: x: 4, y: 4, z: 16 (z_hi: 2, z_lo: 8; z = z_hi * 8 + z_lo), core: 2. Of those that a mesh axis runs over, the one named last changes fastest.
Arguments:
- samples: bfloat16 [16384, 1024], P(('grp', 'dev')), may hold values from -0.1875 to 0.1875
- set_labels: int32 [16384], P(('grp', 'dev')), may hold values 0 or 1
- sign_words: int32 [16384, 25], P(('grp', 'dev')), may hold values from 0 to 2097151
- corpus: bfloat16 [16384, 1024], P(('grp', 'dev')), may hold values from -0.1875 to 0.1875
- scale_grid: float32 [16], replicated, may hold values from 0.25 to 4
- scale_pick: int32 [4], replicated, may hold values from 0 to 15
Outputs:
- quad_forms: float32 [4, 512], replicated
- test_scores: float32 [4], replicated
- proof: float32 [4, 16384], P(None, ('grp', 'dev'))
The draws below stay inside these ranges and needn't reach their ends.
Inputs may be any that keep to these rules, and one draw needn't show every extreme that they name: `sign_words`: every word is below 2 ** 21; each of its 21 bits is a sign, 1 for +1 and 0 for -1. `scale_pick`: indices into the grid, from 0 to 15.
All inputs are finite; a program needn't handle non-finite values. No bound on the sum of `set_labels` on one device may be relied on, other than what follows from the above.
Results may differ from the reference program's by a relative error of at most 0.0099.
Values may be sent and summed in bfloat16 or wider, within the bound.
No kernel may reach another device: no remote copies, remote signals or barrier semaphores. Data moves between devices by JAX's collectives and lax.ppermute only.
A program may use at most 64 MiB of HBM per device.

```python
import math
import jax
import jax.numpy as jnp
from jax import lax

D = 1024
NB = 4
GRID = 16
BOOT = 511
WORDS = 25
M = 16384
CORPUS = 16384
N_GRP = 16


def set_ends(result, rng, least, top_value):
    longest = result.shape.index(max(result.shape))
    spots = []
    for shift in (0, 1):
        where = [jax.random.randint(jax.random.fold_in(rng, axis), (), 0, length) for axis, length in enumerate(result.shape)]
        where[longest] = (where[longest] + shift) % result.shape[longest]
        spots.append(tuple(where))
    return result.at[spots[0]].set(least).at[spots[1]].set(top_value)


def level_of(key, dims, split, smallest, top_value):
    gain, own = 1.0, jax.random.fold_in(key, 6)
    for axis_at, shards_of in split:
        heights = jnp.exp(jax.random.uniform(jax.random.fold_in(own, axis_at), (shards_of,), jnp.float32, smallest / len(split), top_value / len(split)))
        gain = gain * jnp.repeat(heights, dims[axis_at] // shards_of).reshape([-1 if axis == axis_at else 1 for axis in range(len(dims))])
    return gain


def scatter_about(own_key, shape, scale, reach, cuts=(), kind=jnp.bfloat16):
    result = scale * jax.random.normal(own_key, shape, jnp.float32)
    if cuts:
        result = result * level_of(own_key, shape, cuts, -0.22, 0.18)
    return jnp.clip(result, -reach, reach).astype(kind)


def setup_inputs(seed: int = 0) -> dict:
    keys = jax.random.split(jax.random.key(seed), 7)
    samples = scatter_about(keys[0], (M, D), (D ** -0.5), 0.1875, ((0, 512),))
    set_labels = set_ends((jax.random.randint(keys[1], (M,), 0, 2) < 1).astype(jnp.int32), jax.random.fold_in(keys[1], 1), 0, 1)
    sign_words = set_ends(jax.random.randint(keys[2], (M, WORDS), 0, 2097152), jax.random.fold_in(keys[2], 1), 0, 2097151).astype(jnp.int32)
    corpus = scatter_about(keys[3], (CORPUS, D), (D ** -0.5), 0.1875, ((0, 512),))
    scale_grid = jnp.clip(jnp.exp(jax.random.uniform(keys[4], (GRID,), jnp.float32, math.log(0.25), math.log(4.0))), 0.25, 4.0)
    scale_pick = set_ends(jax.random.randint(keys[5], (NB,), 0, GRID), jax.random.fold_in(keys[5], 1), 0, GRID - 1).astype(jnp.int32)
    return dict(samples=samples, set_labels=set_labels, sign_words=sign_words, corpus=corpus, scale_grid=scale_grid, scale_pick=scale_pick)


word_bits = 21

def make_vectors(set_labels, sign_words):
    weights = (1 - 2 * set_labels).astype(jnp.float32)
    shifts = jnp.arange(word_bits, dtype=jnp.int32)
    bit_flags = jnp.right_shift(sign_words[:, :, None], shifts[None, None, :]) & 1
    bit_flags = bit_flags.reshape(sign_words.shape[0], -1)[:, :BOOT]
    sign_values = (2 * bit_flags - 1).astype(jnp.float32)
    vectors = jnp.concatenate([weights[:, None], sign_values * weights[:, None]], axis=1)
    return vectors.astype(jnp.bfloat16)

def band_scales(scale_grid, scale_pick):
    onehot = (scale_pick[:, None] == jnp.arange(scale_grid.shape[0], dtype=jnp.int32)[None, :]).astype(jnp.float32)
    chosen = lax.optimization_barrier(jnp.sum(onehot * scale_grid[None, :], axis=1))
    return 0.5 / chosen

def rounded(values):
    narrow = values.astype(jnp.bfloat16)
    narrow = lax.optimization_barrier(narrow)
    return narrow.astype(jnp.float32)

def reference(samples, set_labels, sign_words, corpus, scale_grid, scale_pick):
    vectors = make_vectors(set_labels, sign_words).astype(jnp.float32)
    scales = band_scales(scale_grid, scale_pick)
    samples_wide = samples.astype(jnp.float32)
    corpus_wide = corpus.astype(jnp.float32)
    sample_sq = lax.optimization_barrier(jnp.sum(samples_wide * samples_wide, axis=1))
    corpus_sq = lax.optimization_barrier(jnp.sum(corpus_wide * corpus_wide, axis=1))
    total = samples.shape[0]
    span = total // N_GRP
    corpus_span = corpus.shape[0] // N_GRP
    weights = vectors[:, 0]

    def test_block(block_id):
        offset = (block_id * span).astype(jnp.int32)
        block_rows = lax.dynamic_slice_in_dim(samples_wide, offset, span, 0)
        block_sq = lax.dynamic_slice_in_dim(sample_sq, offset, span, 0)
        block_vec = lax.dynamic_slice_in_dim(vectors, offset, span, 0)
        cross = jnp.dot(block_rows, samples_wide.T, precision=lax.Precision.HIGHEST)
        dist = block_sq[:, None] + sample_sq[None, :] - 2.0 * cross
        results = []
        for kernel_id in range(NB):
            kern = rounded(jnp.exp(-dist * scales[kernel_id]))
            product = jnp.dot(kern, vectors, precision=lax.Precision.HIGHEST)
            results.append(lax.optimization_barrier(jnp.sum(block_vec * product, axis=0)))
        return jnp.stack(results)
    partial_forms = lax.map(test_block, jnp.arange(N_GRP, dtype=jnp.int32))
    quad_forms = lax.optimization_barrier(jnp.sum(partial_forms, axis=0)) / total
    bootstrap = quad_forms[:, 1:]
    centre = lax.optimization_barrier(jnp.mean(bootstrap, axis=1))
    spread = lax.optimization_barrier(jnp.mean(jnp.square(bootstrap - centre[:, None]), axis=1))
    test_scores = (quad_forms[:, 0] - centre) / jnp.sqrt(spread + 1e-06)

    def proof_block(block_id):
        offset = (block_id * corpus_span).astype(jnp.int32)
        block_rows = lax.dynamic_slice_in_dim(corpus_wide, offset, corpus_span, 0)
        block_sq = lax.dynamic_slice_in_dim(corpus_sq, offset, corpus_span, 0)
        cross = jnp.dot(block_rows, samples_wide.T, precision=lax.Precision.HIGHEST)
        dist = block_sq[:, None] + sample_sq[None, :] - 2.0 * cross
        results = []
        for kernel_id in range(NB):
            kern = rounded(jnp.exp(-dist * scales[kernel_id]))
            results.append(jnp.dot(kern, weights, precision=lax.Precision.HIGHEST))
        return jnp.stack(results)
    proof_parts = lax.map(proof_block, jnp.arange(N_GRP, dtype=jnp.int32))
    proof = jnp.transpose(proof_parts, (1, 0, 2)).reshape(NB, corpus.shape[0])
    inv_root = jnp.float32(1.0) / jnp.sqrt(jnp.float32(total))
    proof = proof * inv_root
    return (quad_forms, test_scores, proof)
```

```python
import numpy as np
import jax
import jax.numpy as jnp
from jax import lax
from jax.sharding import PartitionSpec as P

NB = 4
BOOT = 511
D = 1024
META = 128
CHUNK = 7


word_bits = 21


def make_vectors(set_labels, sign_words):
    weights = (1 - 2 * set_labels).astype(jnp.float32)
    shifts = jnp.arange(word_bits, dtype=jnp.int32)
    bit_flags = jnp.right_shift(sign_words[:, :, None], shifts[None, None, :]) & 1
    bit_flags = bit_flags.reshape(sign_words.shape[0], -1)[:, :BOOT]
    sign_values = (2 * bit_flags - 1).astype(jnp.float32)
    vectors = jnp.concatenate([weights[:, None], sign_values * weights[:, None]], axis=1)
    return vectors.astype(jnp.bfloat16)


def band_scales(scale_grid, scale_pick):
    onehot = (
        scale_pick[:, None] == jnp.arange(scale_grid.shape[0], dtype=jnp.int32)[None, :]
    ).astype(jnp.float32)
    chosen = jnp.sum(onehot * scale_grid[None, :], axis=1)
    return 0.5 / chosen


def squares(matrix):
    wide = matrix.astype(jnp.float32)
    return jnp.sum(wide * wide, axis=1)


def distances(left, left_sq, right, right_sq):
    cross = lax.dot_general(
        left, right, (((1,), (1,)), ((), ())), preferred_element_type=jnp.float32
    )
    return left_sq[:, None] + right_sq[None, :] - 2.0 * cross


def pack_meta(set_labels, sign_words):
    words = sign_words.shape[1]
    chunks = [(sign_words >> (CHUNK * c)) & ((1 << CHUNK) - 1) for c in range(3)]
    meta = jnp.concatenate([set_labels[:, None]] + chunks, axis=1)
    pad = META - meta.shape[1]
    meta = jnp.pad(meta, ((0, 0), (0, pad)))
    return meta.astype(jnp.bfloat16), words


def unpack(buf, words):
    rows = buf[:, :D]
    meta = buf[:, D:D + 1 + 3 * words].astype(jnp.float32).astype(jnp.int32)
    labels = meta[:, 0]
    c = [meta[:, 1 + k * words:1 + (k + 1) * words] for k in range(3)]
    sign_words = c[0] + (c[1] << CHUNK) + (c[2] << (2 * CHUNK))
    return rows, make_vectors(labels, sign_words)


def xor_gather(x, axis, n, bits):
    idx = lax.axis_index(axis)
    buf = x[None]
    for b in bits:
        k = 1 << b
        other = lax.ppermute(buf, axis, [(i, i ^ k) for i in range(n)])
        lo = (idx & k) == 0
        buf = jnp.where(lo, jnp.concatenate([buf, other]), jnp.concatenate([other, buf]))
    order = [sum(((t >> j) & 1) << b for j, b in enumerate(bits)) for t in range(n)]
    return buf, order


def per_device(samples, set_labels, sign_words, corpus, scale_grid, scale_pick):
    scales = band_scales(scale_grid, scale_pick)
    n_grp = lax.axis_size("grp")
    n_dev = lax.axis_size("dev")
    rows_here = samples.shape[0]
    total = rows_here * n_grp * n_dev
    inv_root = jnp.float32(1.0) / jnp.sqrt(jnp.float32(total))

    meta, words = pack_meta(set_labels, sign_words)
    own = jnp.concatenate([samples, meta], axis=1)
    own_wide = jnp.concatenate([own, corpus], axis=1)

    grp_bits = [b for b in range(1, n_grp.bit_length() - 1)] + [0]
    dev_bits = list(range(n_dev.bit_length() - 1))
    col_buf, col_order = xor_gather(own_wide, "grp", n_grp, grp_bits)
    blk_buf, _ = xor_gather(own, "dev", n_dev, dev_bits)

    col_buf = col_buf.reshape(n_grp * rows_here, -1)
    blk_buf = blk_buf.reshape(n_dev * rows_here, -1)
    col_rows, col_vec = unpack(col_buf[:, :D + META], words)
    col_corpus = col_buf[:, D + META:]
    block_rows, block_vec = unpack(blk_buf, words)

    col_sq = squares(col_rows)
    block_sq = squares(block_rows)

    dist = distances(block_rows, block_sq, col_rows, col_sq)
    block_wide = block_vec.astype(jnp.float32)
    forms = []
    for kernel_id in range(NB):
        kern = jnp.exp(-dist * scales[kernel_id]).astype(jnp.bfloat16)
        product = jnp.dot(kern, col_vec, preferred_element_type=jnp.float32)
        forms.append(jnp.sum(block_wide * product, axis=0))
    forms_part = jnp.stack(forms)

    cdist = distances(col_corpus, squares(col_corpus), block_rows, block_sq)
    weights = block_vec[:, 0]
    proofs = []
    for kernel_id in range(NB):
        kern = jnp.exp(-cdist * scales[kernel_id]).astype(jnp.bfloat16)
        proofs.append(jnp.dot(kern, weights, preferred_element_type=jnp.float32))
    proof_part = jnp.stack(proofs).reshape(NB, n_grp, rows_here)
    inverse = np.argsort(np.array(col_order))
    proof_part = jnp.take(proof_part, jnp.asarray(inverse, jnp.int32), axis=1)
    proof_part = jnp.transpose(proof_part, (1, 0, 2))
    got = lax.all_to_all(proof_part, "grp", 0, 0, tiled=True)
    proof = jnp.sum(got, axis=0) * inv_root

    quad_forms = lax.psum(forms_part, ("grp", "dev")) / total
    bootstrap = quad_forms[:, 1:]
    centre = jnp.mean(bootstrap, axis=1)
    spread = jnp.mean(jnp.square(bootstrap - centre[:, None]), axis=1)
    test_scores = (quad_forms[:, 0] - centre) / jnp.sqrt(spread + 1e-06)
    return (quad_forms, test_scores, proof)


def solution(mesh):
    in_specs = (
        P(("grp", "dev"), None),
        P(("grp", "dev")),
        P(("grp", "dev"), None),
        P(("grp", "dev"), None),
        P(),
        P(),
    )
    out_specs = (P(), P(), P(None, ("grp", "dev")))
    return jax.shard_map(
        per_device, mesh=mesh, in_specs=in_specs, out_specs=out_specs, check_vma=False
    )
```

```python
import numpy as np
import jax
import jax.numpy as jnp
from jax import lax
from jax.sharding import PartitionSpec as P

NB = 4
BOOT = 511
D = 1024
META = 128
CHUNK = 7


word_bits = 21


def make_vectors(set_labels, sign_words):
    weights = (1 - 2 * set_labels).astype(jnp.float32)
    shifts = jnp.arange(word_bits, dtype=jnp.int32)
    bit_flags = jnp.right_shift(sign_words[:, :, None], shifts[None, None, :]) & 1
    bit_flags = bit_flags.reshape(sign_words.shape[0], -1)[:, :BOOT]
    sign_values = (2 * bit_flags - 1).astype(jnp.float32)
    vectors = jnp.concatenate([weights[:, None], sign_values * weights[:, None]], axis=1)
    return vectors.astype(jnp.bfloat16)


def band_scales(scale_grid, scale_pick):
    onehot = (
        scale_pick[:, None] == jnp.arange(scale_grid.shape[0], dtype=jnp.int32)[None, :]
    ).astype(jnp.float32)
    chosen = jnp.sum(onehot * scale_grid[None, :], axis=1)
    return 0.5 / chosen


def squares(matrix):
    wide = matrix.astype(jnp.float32)
    return jnp.sum(wide * wide, axis=1)


def distances(left, left_sq, right, right_sq):
    cross = lax.dot_general(
        left, right, (((1,), (1,)), ((), ())), preferred_element_type=jnp.float32
    )
    return left_sq[:, None] + right_sq[None, :] - 2.0 * cross


def pack_meta(set_labels, sign_words):
    words = sign_words.shape[1]
    chunks = [(sign_words >> (CHUNK * c)) & ((1 << CHUNK) - 1) for c in range(3)]
    meta = jnp.concatenate([set_labels[:, None]] + chunks, axis=1)
    pad = META - meta.shape[1]
    meta = jnp.pad(meta, ((0, 0), (0, pad)))
    return meta.astype(jnp.bfloat16), words


def unpack(buf, words):
    rows = buf[:, :D]
    meta = buf[:, D:D + 1 + 3 * words].astype(jnp.float32).astype(jnp.int32)
    labels = meta[:, 0]
    c = [meta[:, 1 + k * words:1 + (k + 1) * words] for k in range(3)]
    sign_words = c[0] + (c[1] << CHUNK) + (c[2] << (2 * CHUNK))
    return rows, make_vectors(labels, sign_words)


def xor_gather(x, axis, n, bits):
    idx = lax.axis_index(axis)
    buf = x[None]
    for b in bits:
        k = 1 << b
        other = lax.ppermute(buf, axis, [(i, i ^ k) for i in range(n)])
        lo = (idx & k) == 0
        buf = jnp.where(lo, jnp.concatenate([buf, other]), jnp.concatenate([other, buf]))
    order = [sum(((t >> j) & 1) << b for j, b in enumerate(bits)) for t in range(n)]
    return buf, order


GRP_ORDER = (3, 1, 2, 0)
DEV_ORDER = (2, 4, 1, 0, 3)
SUM_ORDER = (("grp", 0), ("dev", 0), ("dev", 1), ("dev", 2), ("grp", 1), ("grp", 2), ("dev", 3), ("dev", 4), ("grp", 3))


def axis_order(n, preferred):
    nbits = n.bit_length() - 1
    bits = [b for b in preferred if b < nbits]
    return bits + [b for b in range(nbits) if b not in bits]


def xor_sum(x, n_grp, n_dev):
    sizes = {"grp": n_grp, "dev": n_dev}
    steps = [(a, b) for a, b in SUM_ORDER if (1 << b) < sizes[a]]
    for a in sizes:
        steps += [(a, b) for b in range(sizes[a].bit_length() - 1) if (a, b) not in steps]
    for a, b in steps:
        k = 1 << b
        x = x + lax.ppermute(x, a, [(i, i ^ k) for i in range(sizes[a])])
    return x


def per_device(samples, set_labels, sign_words, corpus, scale_grid, scale_pick):
    scales = band_scales(scale_grid, scale_pick)
    n_grp = lax.axis_size("grp")
    n_dev = lax.axis_size("dev")
    rows_here = samples.shape[0]
    total = rows_here * n_grp * n_dev
    inv_root = jnp.float32(1.0) / jnp.sqrt(jnp.float32(total))

    meta, words = pack_meta(set_labels, sign_words)
    own = jnp.concatenate([samples, meta], axis=1)
    own_wide = jnp.concatenate([own, corpus], axis=1)

    grp_bits = axis_order(n_grp, GRP_ORDER)
    dev_bits = axis_order(n_dev, DEV_ORDER)
    col_buf, col_order = xor_gather(own_wide, "grp", n_grp, grp_bits)
    blk_buf, _ = xor_gather(own, "dev", n_dev, dev_bits)

    col_buf = col_buf.reshape(n_grp * rows_here, -1)
    blk_buf = blk_buf.reshape(n_dev * rows_here, -1)
    col_rows, col_vec = unpack(col_buf[:, :D + META], words)
    col_corpus = col_buf[:, D + META:]
    block_rows, block_vec = unpack(blk_buf, words)

    col_sq = squares(col_rows)
    block_sq = squares(block_rows)

    dist = distances(block_rows, block_sq, col_rows, col_sq)
    block_wide = block_vec.astype(jnp.float32)
    forms = []
    for kernel_id in range(NB):
        kern = jnp.exp(-dist * scales[kernel_id]).astype(jnp.bfloat16)
        product = jnp.dot(kern, col_vec, preferred_element_type=jnp.float32)
        forms.append(jnp.sum(block_wide * product, axis=0))
    forms_part = jnp.stack(forms)

    cdist = distances(col_corpus, squares(col_corpus), block_rows, block_sq)
    weights = block_vec[:, 0]
    proofs = []
    for kernel_id in range(NB):
        kern = jnp.exp(-cdist * scales[kernel_id]).astype(jnp.bfloat16)
        proofs.append(jnp.dot(kern, weights, preferred_element_type=jnp.float32))
    proof_part = jnp.stack(proofs).reshape(NB, n_grp, rows_here)
    inverse = np.argsort(np.array(col_order))
    proof_part = jnp.take(proof_part, jnp.asarray(inverse, jnp.int32), axis=1)
    proof_part = jnp.transpose(proof_part, (1, 0, 2))
    got = lax.all_to_all(proof_part, "grp", 0, 0, tiled=True)
    proof = jnp.sum(got, axis=0) * inv_root

    quad_forms = xor_sum(forms_part, n_grp, n_dev) / total
    bootstrap = quad_forms[:, 1:]
    centre = jnp.mean(bootstrap, axis=1)
    spread = jnp.mean(jnp.square(bootstrap - centre[:, None]), axis=1)
    test_scores = (quad_forms[:, 0] - centre) / jnp.sqrt(spread + 1e-06)
    return (quad_forms, test_scores, proof)


def solution(mesh):
    in_specs = (
        P(("grp", "dev"), None),
        P(("grp", "dev")),
        P(("grp", "dev"), None),
        P(("grp", "dev"), None),
        P(),
        P(),
    )
    out_specs = (P(), P(), P(None, ("grp", "dev")))
    return jax.shard_map(
        per_device, mesh=mesh, in_specs=in_specs, out_specs=out_specs, check_vma=False
    )
```

```python
import numpy as np
import jax
import jax.numpy as jnp
from jax import lax
from jax.sharding import PartitionSpec as P

NB = 4
BOOT = 511
D = 1024
META = 128
CHUNK = 7


word_bits = 21


def make_vectors(set_labels, sign_words):
    weights = (1 - 2 * set_labels).astype(jnp.float32)
    shifts = jnp.arange(word_bits, dtype=jnp.int32)
    bit_flags = jnp.right_shift(sign_words[:, :, None], shifts[None, None, :]) & 1
    bit_flags = bit_flags.reshape(sign_words.shape[0], -1)[:, :BOOT]
    sign_values = (2 * bit_flags - 1).astype(jnp.float32)
    vectors = jnp.concatenate([weights[:, None], sign_values * weights[:, None]], axis=1)
    return vectors.astype(jnp.bfloat16)


def band_scales(scale_grid, scale_pick):
    onehot = (
        scale_pick[:, None] == jnp.arange(scale_grid.shape[0], dtype=jnp.int32)[None, :]
    ).astype(jnp.float32)
    chosen = jnp.sum(onehot * scale_grid[None, :], axis=1)
    return 0.5 / chosen


def squares(matrix):
    wide = matrix.astype(jnp.float32)
    return jnp.sum(wide * wide, axis=1)


def distances(left, left_sq, right, right_sq):
    cross = lax.dot_general(
        left, right, (((1,), (1,)), ((), ())), preferred_element_type=jnp.float32
    )
    return left_sq[:, None] + right_sq[None, :] - 2.0 * cross


def pack_meta(set_labels, sign_words):
    words = sign_words.shape[1]
    chunks = [(sign_words >> (CHUNK * c)) & ((1 << CHUNK) - 1) for c in range(3)]
    meta = jnp.concatenate([set_labels[:, None]] + chunks, axis=1)
    pad = META - meta.shape[1]
    meta = jnp.pad(meta, ((0, 0), (0, pad)))
    return meta.astype(jnp.bfloat16), words


def unpack(buf, words):
    rows = buf[:, :D]
    meta = buf[:, D:D + 1 + 3 * words].astype(jnp.float32).astype(jnp.int32)
    labels = meta[:, 0]
    c = [meta[:, 1 + k * words:1 + (k + 1) * words] for k in range(3)]
    sign_words = c[0] + (c[1] << CHUNK) + (c[2] << (2 * CHUNK))
    return rows, make_vectors(labels, sign_words)


def xor_gather(x, axis, n, bits):
    idx = lax.axis_index(axis)
    buf = x[None]
    for b in bits:
        k = 1 << b
        other = lax.ppermute(buf, axis, [(i, i ^ k) for i in range(n)])
        lo = (idx & k) == 0
        buf = jnp.where(lo, jnp.concatenate([buf, other]), jnp.concatenate([other, buf]))
    order = [sum(((t >> j) & 1) << b for j, b in enumerate(bits)) for t in range(n)]
    return buf, order


GRP_ORDER = (3, 1, 2, 0)
DEV_ORDER = (2, 4, 1, 0, 3)
SUM_ROUNDS = (("grp", 0, 1), ("dev", 0, 3), ("dev", 3, 2), ("grp", 1, 2), ("grp", 3, 1))


def axis_order(n, preferred):
    nbits = n.bit_length() - 1
    bits = [b for b in preferred if b < nbits]
    return bits + [b for b in range(nbits) if b not in bits]


def xor_sum(x, n_grp, n_dev):
    sizes = {"grp": n_grp, "dev": n_dev}
    rounds = []
    for a, lo, width in SUM_ROUNDS:
        nbits = sizes[a].bit_length() - 1
        width = min(width, nbits - lo)
        if width > 0:
            rounds.append((a, lo, width))
    for a in sizes:
        seen = {b for r in rounds if r[0] == a for b in range(r[1], r[1] + r[2])}
        rounds += [(a, b, 1) for b in range(sizes[a].bit_length() - 1) if b not in seen]
    for a, lo, width in rounds:
        r = 1 << width
        n = sizes[a]
        got = [x] + [lax.ppermute(x, a, [(i, i ^ (k << lo)) for i in range(n)]) for k in range(1, r)]
        got = jnp.stack(got)
        mine = (lax.axis_index(a) >> lo) & (r - 1)
        got = jnp.take(got, jnp.arange(r, dtype=jnp.int32) ^ mine, axis=0)
        x = got[0]
        for j in range(1, r):
            x = x + got[j]
    return x


def per_device(samples, set_labels, sign_words, corpus, scale_grid, scale_pick):
    scales = band_scales(scale_grid, scale_pick)
    n_grp = lax.axis_size("grp")
    n_dev = lax.axis_size("dev")
    rows_here = samples.shape[0]
    total = rows_here * n_grp * n_dev
    inv_root = jnp.float32(1.0) / jnp.sqrt(jnp.float32(total))

    meta, words = pack_meta(set_labels, sign_words)
    own = jnp.concatenate([samples, meta], axis=1)
    own_wide = jnp.concatenate([own, corpus], axis=1)

    grp_bits = axis_order(n_grp, GRP_ORDER)
    dev_bits = axis_order(n_dev, DEV_ORDER)
    col_buf, col_order = xor_gather(own_wide, "grp", n_grp, grp_bits)
    blk_buf, _ = xor_gather(own, "dev", n_dev, dev_bits)

    col_buf = col_buf.reshape(n_grp * rows_here, -1)
    blk_buf = blk_buf.reshape(n_dev * rows_here, -1)
    col_rows, col_vec = unpack(col_buf[:, :D + META], words)
    col_corpus = col_buf[:, D + META:]
    block_rows, block_vec = unpack(blk_buf, words)

    col_sq = squares(col_rows)
    block_sq = squares(block_rows)

    dist = distances(block_rows, block_sq, col_rows, col_sq)
    block_wide = block_vec.astype(jnp.float32)
    forms = []
    for kernel_id in range(NB):
        kern = jnp.exp(-dist * scales[kernel_id]).astype(jnp.bfloat16)
        product = jnp.dot(kern, col_vec, preferred_element_type=jnp.float32)
        forms.append(jnp.sum(block_wide * product, axis=0))
    forms_part = jnp.stack(forms)

    cdist = distances(col_corpus, squares(col_corpus), block_rows, block_sq)
    weights = block_vec[:, 0]
    proofs = []
    for kernel_id in range(NB):
        kern = jnp.exp(-cdist * scales[kernel_id]).astype(jnp.bfloat16)
        proofs.append(jnp.dot(kern, weights, preferred_element_type=jnp.float32))
    proof_part = jnp.stack(proofs).reshape(NB, n_grp, rows_here)
    inverse = np.argsort(np.array(col_order))
    proof_part = jnp.take(proof_part, jnp.asarray(inverse, jnp.int32), axis=1)
    proof_part = jnp.transpose(proof_part, (1, 0, 2))
    got = lax.all_to_all(proof_part, "grp", 0, 0, tiled=True)
    proof = jnp.sum(got, axis=0) * inv_root

    quad_forms = xor_sum(forms_part, n_grp, n_dev) / total
    bootstrap = quad_forms[:, 1:]
    centre = jnp.mean(bootstrap, axis=1)
    spread = jnp.mean(jnp.square(bootstrap - centre[:, None]), axis=1)
    test_scores = (quad_forms[:, 0] - centre) / jnp.sqrt(spread + 1e-06)
    return (quad_forms, test_scores, proof)


def solution(mesh):
    in_specs = (
        P(("grp", "dev"), None),
        P(("grp", "dev")),
        P(("grp", "dev"), None),
        P(("grp", "dev"), None),
        P(),
        P(),
    )
    out_specs = (P(), P(), P(None, ("grp", "dev")))
    return jax.shard_map(
        per_device, mesh=mesh, in_specs=in_specs, out_specs=out_specs, check_vma=False
    )
```

```python
import numpy as np
import jax
import jax.numpy as jnp
from jax import lax
from jax.sharding import PartitionSpec as P

NB = 4
BOOT = 511
D = 1024
META = 128
CHUNK = 7


word_bits = 21


def make_vectors(set_labels, sign_words):
    weights = (1 - 2 * set_labels).astype(jnp.float32)
    shifts = jnp.arange(word_bits, dtype=jnp.int32)
    bit_flags = jnp.right_shift(sign_words[:, :, None], shifts[None, None, :]) & 1
    bit_flags = bit_flags.reshape(sign_words.shape[0], -1)[:, :BOOT]
    sign_values = (2 * bit_flags - 1).astype(jnp.float32)
    vectors = jnp.concatenate([weights[:, None], sign_values * weights[:, None]], axis=1)
    return vectors.astype(jnp.bfloat16)


def band_scales(scale_grid, scale_pick):
    onehot = (
        scale_pick[:, None] == jnp.arange(scale_grid.shape[0], dtype=jnp.int32)[None, :]
    ).astype(jnp.float32)
    chosen = jnp.sum(onehot * scale_grid[None, :], axis=1)
    return 0.5 / chosen


def squares(matrix):
    wide = matrix.astype(jnp.float32)
    return jnp.sum(wide * wide, axis=1)


def distances(left, left_sq, right, right_sq):
    cross = lax.dot_general(
        left, right, (((1,), (1,)), ((), ())), preferred_element_type=jnp.float32
    )
    return left_sq[:, None] + right_sq[None, :] - 2.0 * cross


def pack_meta(set_labels, sign_words):
    words = sign_words.shape[1]
    chunks = [(sign_words >> (CHUNK * c)) & ((1 << CHUNK) - 1) for c in range(3)]
    meta = jnp.concatenate([set_labels[:, None]] + chunks, axis=1)
    pad = META - meta.shape[1]
    meta = jnp.pad(meta, ((0, 0), (0, pad)))
    return meta.astype(jnp.bfloat16), words


def unpack(buf, words):
    rows = buf[:, :D]
    meta = buf[:, D:D + 1 + 3 * words].astype(jnp.float32).astype(jnp.int32)
    labels = meta[:, 0]
    c = [meta[:, 1 + k * words:1 + (k + 1) * words] for k in range(3)]
    sign_words = c[0] + (c[1] << CHUNK) + (c[2] << (2 * CHUNK))
    return rows, make_vectors(labels, sign_words)


def xor_gather(x, axis, n, bits):
    idx = lax.axis_index(axis)
    buf = x[None]
    for b in bits:
        k = 1 << b
        other = lax.ppermute(buf, axis, [(i, i ^ k) for i in range(n)])
        lo = (idx & k) == 0
        buf = jnp.where(lo, jnp.concatenate([buf, other]), jnp.concatenate([other, buf]))
    order = [sum(((t >> j) & 1) << b for j, b in enumerate(bits)) for t in range(n)]
    return buf, order


GRP_ORDER = (3, 1, 2, 0)
DEV_ORDERS = ((2, 4, 1, 0, 3), (4, 2, 3, 1, 0))
SUM_ORDER = (("grp", 0), ("dev", 0), ("dev", 1), ("dev", 2), ("grp", 1), ("grp", 2), ("dev", 3), ("dev", 4), ("grp", 3))


def axis_order(n, preferred):
    nbits = n.bit_length() - 1
    bits = [b for b in preferred if b < nbits]
    return bits + [b for b in range(nbits) if b not in bits]


def xor_sum(x, n_grp, n_dev):
    sizes = {"grp": n_grp, "dev": n_dev}
    steps = [(a, b) for a, b in SUM_ORDER if (1 << b) < sizes[a]]
    for a in sizes:
        steps += [(a, b) for b in range(sizes[a].bit_length() - 1) if (a, b) not in steps]
    for a, b in steps:
        k = 1 << b
        x = x + lax.ppermute(x, a, [(i, i ^ k) for i in range(sizes[a])])
    return x


def per_device(samples, set_labels, sign_words, corpus, scale_grid, scale_pick):
    scales = band_scales(scale_grid, scale_pick)
    n_grp = lax.axis_size("grp")
    n_dev = lax.axis_size("dev")
    rows_here = samples.shape[0]
    total = rows_here * n_grp * n_dev
    inv_root = jnp.float32(1.0) / jnp.sqrt(jnp.float32(total))

    meta, words = pack_meta(set_labels, sign_words)
    own = jnp.concatenate([samples, meta], axis=1)
    own_wide = jnp.concatenate([own, corpus], axis=1)

    grp_bits = axis_order(n_grp, GRP_ORDER)
    halves = [own[: rows_here // 2], own[rows_here // 2:]]
    col_buf, col_order = xor_gather(own_wide, "grp", n_grp, grp_bits)
    blk_buf = jnp.concatenate(
        [xor_gather(h, "dev", n_dev, axis_order(n_dev, o))[0] for h, o in zip(halves, DEV_ORDERS)], axis=1
    )

    col_buf = col_buf.reshape(n_grp * rows_here, -1)
    blk_buf = blk_buf.reshape(n_dev * rows_here, -1)
    col_rows, col_vec = unpack(col_buf[:, :D + META], words)
    col_corpus = col_buf[:, D + META:]
    block_rows, block_vec = unpack(blk_buf, words)

    col_sq = squares(col_rows)
    block_sq = squares(block_rows)

    dist = distances(block_rows, block_sq, col_rows, col_sq)
    block_wide = block_vec.astype(jnp.float32)
    forms = []
    for kernel_id in range(NB):
        kern = jnp.exp(-dist * scales[kernel_id]).astype(jnp.bfloat16)
        product = jnp.dot(kern, col_vec, preferred_element_type=jnp.float32)
        forms.append(jnp.sum(block_wide * product, axis=0))
    forms_part = jnp.stack(forms)

    cdist = distances(col_corpus, squares(col_corpus), block_rows, block_sq)
    weights = block_vec[:, 0]
    proofs = []
    for kernel_id in range(NB):
        kern = jnp.exp(-cdist * scales[kernel_id]).astype(jnp.bfloat16)
        proofs.append(jnp.dot(kern, weights, preferred_element_type=jnp.float32))
    proof_part = jnp.stack(proofs).reshape(NB, n_grp, rows_here)
    inverse = np.argsort(np.array(col_order))
    proof_part = jnp.take(proof_part, jnp.asarray(inverse, jnp.int32), axis=1)
    proof_part = jnp.transpose(proof_part, (1, 0, 2))
    got = lax.all_to_all(proof_part, "grp", 0, 0, tiled=True)
    proof = jnp.sum(got, axis=0) * inv_root

    quad_forms = xor_sum(forms_part, n_grp, n_dev) / total
    bootstrap = quad_forms[:, 1:]
    centre = jnp.mean(bootstrap, axis=1)
    spread = jnp.mean(jnp.square(bootstrap - centre[:, None]), axis=1)
    test_scores = (quad_forms[:, 0] - centre) / jnp.sqrt(spread + 1e-06)
    return (quad_forms, test_scores, proof)


def solution(mesh):
    in_specs = (
        P(("grp", "dev"), None),
        P(("grp", "dev")),
        P(("grp", "dev"), None),
        P(("grp", "dev"), None),
        P(),
        P(),
    )
    out_specs = (P(), P(), P(None, ("grp", "dev")))
    return jax.shard_map(
        per_device, mesh=mesh, in_specs=in_specs, out_specs=out_specs, check_vma=False
    )
```

```python
import numpy as np
import jax
import jax.numpy as jnp
from jax import lax
from jax.sharding import PartitionSpec as P

NB = 4
BOOT = 511
D = 1024
META = 128
CHUNK = 7


word_bits = 21


def make_vectors(set_labels, sign_words):
    weights = (1 - 2 * set_labels).astype(jnp.float32)
    shifts = jnp.arange(word_bits, dtype=jnp.int32)
    bit_flags = jnp.right_shift(sign_words[:, :, None], shifts[None, None, :]) & 1
    bit_flags = bit_flags.reshape(sign_words.shape[0], -1)[:, :BOOT]
    sign_values = (2 * bit_flags - 1).astype(jnp.float32)
    vectors = jnp.concatenate([weights[:, None], sign_values * weights[:, None]], axis=1)
    return vectors.astype(jnp.bfloat16)


def band_scales(scale_grid, scale_pick):
    onehot = (
        scale_pick[:, None] == jnp.arange(scale_grid.shape[0], dtype=jnp.int32)[None, :]
    ).astype(jnp.float32)
    chosen = jnp.sum(onehot * scale_grid[None, :], axis=1)
    return 0.5 / chosen


def squares(matrix):
    wide = matrix.astype(jnp.float32)
    return jnp.sum(wide * wide, axis=1)


def distances(left, left_sq, right, right_sq):
    cross = lax.dot_general(
        left, right, (((1,), (1,)), ((), ())), preferred_element_type=jnp.float32
    )
    return left_sq[:, None] + right_sq[None, :] - 2.0 * cross


def pack_meta(set_labels, sign_words):
    words = sign_words.shape[1]
    chunks = [(sign_words >> (CHUNK * c)) & ((1 << CHUNK) - 1) for c in range(3)]
    meta = jnp.concatenate([set_labels[:, None]] + chunks, axis=1)
    pad = META - meta.shape[1]
    meta = jnp.pad(meta, ((0, 0), (0, pad)))
    return meta.astype(jnp.bfloat16), words


def unpack(buf, words):
    rows = buf[:, :D]
    meta = buf[:, D:D + 1 + 3 * words].astype(jnp.float32).astype(jnp.int32)
    labels = meta[:, 0]
    c = [meta[:, 1 + k * words:1 + (k + 1) * words] for k in range(3)]
    sign_words = c[0] + (c[1] << CHUNK) + (c[2] << (2 * CHUNK))
    return rows, make_vectors(labels, sign_words)


def xor_gather(x, axis, n, bits):
    buf = x[None]
    for b in bits:
        other = lax.ppermute(buf, axis, [(i, i ^ (1 << b)) for i in range(n)])
        buf = jnp.concatenate([buf, other])
    order = [sum(((t >> j) & 1) << b for j, b in enumerate(bits)) for t in range(n)]
    return buf, order


GRP_ORDER = (3, 1, 2, 0)
DEV_ORDERS = ((2, 4, 1, 0, 3), (4, 2, 3, 1, 0))
SUM_ORDER = (("grp", 0), ("dev", 0), ("dev", 1), ("dev", 2), ("grp", 1), ("grp", 2), ("dev", 3), ("dev", 4), ("grp", 3))


def axis_order(n, preferred):
    nbits = n.bit_length() - 1
    bits = [b for b in preferred if b < nbits]
    return bits + [b for b in range(nbits) if b not in bits]


def xor_sum(x, n_grp, n_dev):
    sizes = {"grp": n_grp, "dev": n_dev}
    steps = [(a, b) for a, b in SUM_ORDER if (1 << b) < sizes[a]]
    for a in sizes:
        steps += [(a, b) for b in range(sizes[a].bit_length() - 1) if (a, b) not in steps]
    for a, b in steps:
        k = 1 << b
        x = x + lax.ppermute(x, a, [(i, i ^ k) for i in range(sizes[a])])
    return x


def per_device(samples, set_labels, sign_words, corpus, scale_grid, scale_pick):
    scales = band_scales(scale_grid, scale_pick)
    n_grp = lax.axis_size("grp")
    n_dev = lax.axis_size("dev")
    rows_here = samples.shape[0]
    total = rows_here * n_grp * n_dev
    inv_root = jnp.float32(1.0) / jnp.sqrt(jnp.float32(total))

    meta, words = pack_meta(set_labels, sign_words)
    own = jnp.concatenate([samples, meta], axis=1)
    own_wide = jnp.concatenate([own, corpus], axis=1)

    grp_bits = axis_order(n_grp, GRP_ORDER)
    halves = [own[: rows_here // 2], own[rows_here // 2:]]
    col_buf, col_order = xor_gather(own_wide, "grp", n_grp, grp_bits)
    blk_buf = jnp.concatenate(
        [xor_gather(h, "dev", n_dev, axis_order(n_dev, o))[0] for h, o in zip(halves, DEV_ORDERS)], axis=1
    )

    col_buf = col_buf.reshape(n_grp * rows_here, -1)
    blk_buf = blk_buf.reshape(n_dev * rows_here, -1)
    col_rows, col_vec = unpack(col_buf[:, :D + META], words)
    col_corpus = col_buf[:, D + META:]
    block_rows, block_vec = unpack(blk_buf, words)

    col_sq = squares(col_rows)
    block_sq = squares(block_rows)

    dist = distances(block_rows, block_sq, col_rows, col_sq)
    block_wide = block_vec.astype(jnp.float32)
    forms = []
    for kernel_id in range(NB):
        kern = jnp.exp(-dist * scales[kernel_id]).astype(jnp.bfloat16)
        product = jnp.dot(kern, col_vec, preferred_element_type=jnp.float32)
        forms.append(jnp.sum(block_wide * product, axis=0))
    forms_part = jnp.stack(forms)

    cdist = distances(col_corpus, squares(col_corpus), block_rows, block_sq)
    weights = block_vec[:, 0]
    proofs = []
    for kernel_id in range(NB):
        kern = jnp.exp(-cdist * scales[kernel_id]).astype(jnp.bfloat16)
        proofs.append(jnp.dot(kern, weights, preferred_element_type=jnp.float32))
    proof_part = jnp.stack(proofs).reshape(NB, n_grp, rows_here)
    inverse = jnp.asarray(np.argsort(np.array(col_order)), jnp.int32)
    place = inverse[jnp.arange(n_grp, dtype=jnp.int32) ^ lax.axis_index("grp")]
    proof_part = jnp.take(proof_part, place, axis=1)
    proof_part = jnp.transpose(proof_part, (1, 0, 2))
    got = lax.all_to_all(proof_part, "grp", 0, 0, tiled=True)
    proof = jnp.sum(got, axis=0) * inv_root

    quad_forms = xor_sum(forms_part, n_grp, n_dev) / total
    bootstrap = quad_forms[:, 1:]
    centre = jnp.mean(bootstrap, axis=1)
    spread = jnp.mean(jnp.square(bootstrap - centre[:, None]), axis=1)
    test_scores = (quad_forms[:, 0] - centre) / jnp.sqrt(spread + 1e-06)
    return (quad_forms, test_scores, proof)


def solution(mesh):
    in_specs = (
        P(("grp", "dev"), None),
        P(("grp", "dev")),
        P(("grp", "dev"), None),
        P(("grp", "dev"), None),
        P(),
        P(),
    )
    out_specs = (P(), P(), P(None, ("grp", "dev")))
    return jax.shard_map(
        per_device, mesh=mesh, in_specs=in_specs, out_specs=out_specs, check_vma=False
    )
```

```python
import numpy as np
import jax
import jax.numpy as jnp
from jax import lax
from jax.sharding import PartitionSpec as P

NB = 4
BOOT = 511
D = 1024
META = 128
CHUNK = 7


word_bits = 21


def make_vectors(set_labels, sign_words):
    weights = (1 - 2 * set_labels).astype(jnp.float32)
    shifts = jnp.arange(word_bits, dtype=jnp.int32)
    bit_flags = jnp.right_shift(sign_words[:, :, None], shifts[None, None, :]) & 1
    bit_flags = bit_flags.reshape(sign_words.shape[0], -1)[:, :BOOT]
    sign_values = (2 * bit_flags - 1).astype(jnp.float32)
    vectors = jnp.concatenate([weights[:, None], sign_values * weights[:, None]], axis=1)
    return vectors.astype(jnp.bfloat16)


def band_scales(scale_grid, scale_pick):
    onehot = (
        scale_pick[:, None] == jnp.arange(scale_grid.shape[0], dtype=jnp.int32)[None, :]
    ).astype(jnp.float32)
    chosen = jnp.sum(onehot * scale_grid[None, :], axis=1)
    return 0.5 / chosen


def squares(matrix):
    wide = matrix.astype(jnp.float32)
    return jnp.sum(wide * wide, axis=1)


def distances(left, left_sq, right, right_sq):
    cross = lax.dot_general(
        left, right, (((1,), (1,)), ((), ())), preferred_element_type=jnp.float32
    )
    return left_sq[:, None] + right_sq[None, :] - 2.0 * cross


def pack_meta(set_labels, sign_words):
    words = sign_words.shape[1]
    chunks = [(sign_words >> (CHUNK * c)) & ((1 << CHUNK) - 1) for c in range(3)]
    meta = jnp.concatenate([set_labels[:, None]] + chunks, axis=1)
    pad = META - meta.shape[1]
    meta = jnp.pad(meta, ((0, 0), (0, pad)))
    return meta.astype(jnp.bfloat16), words


def unpack(buf, words):
    rows = buf[:, :D]
    meta = buf[:, D:D + 1 + 3 * words].astype(jnp.float32).astype(jnp.int32)
    labels = meta[:, 0]
    c = [meta[:, 1 + k * words:1 + (k + 1) * words] for k in range(3)]
    sign_words = c[0] + (c[1] << CHUNK) + (c[2] << (2 * CHUNK))
    return rows, make_vectors(labels, sign_words)


def xor_gather(x, axis, n, bits):
    buf = x[None]
    for b in bits:
        other = lax.ppermute(buf, axis, [(i, i ^ (1 << b)) for i in range(n)])
        buf = jnp.concatenate([buf, other])
    order = [sum(((t >> j) & 1) << b for j, b in enumerate(bits)) for t in range(n)]
    return buf, order


GRP_ORDER = (3, 1, 2, 0)
DEV_ORDERS = ((2, 4, 1, 0, 3), (4, 2, 3, 1, 0))
SUM_ORDER = (("grp", 0), ("dev", 0), ("dev", 1), ("dev", 2), ("grp", 1), ("grp", 2), ("dev", 3), ("dev", 4), ("grp", 3))


def axis_order(n, preferred):
    nbits = n.bit_length() - 1
    bits = [b for b in preferred if b < nbits]
    return bits + [b for b in range(nbits) if b not in bits]


def xor_sum(x, n_grp, n_dev):
    sizes = {"grp": n_grp, "dev": n_dev}
    steps = [(a, b) for a, b in SUM_ORDER if (1 << b) < sizes[a]]
    for a in sizes:
        steps += [(a, b) for b in range(sizes[a].bit_length() - 1) if (a, b) not in steps]
    for a, b in steps:
        k = 1 << b
        x = x + lax.ppermute(x, a, [(i, i ^ k) for i in range(sizes[a])])
    return x


def per_device(samples, set_labels, sign_words, corpus, scale_grid, scale_pick):
    scales = band_scales(scale_grid, scale_pick)
    n_grp = lax.axis_size("grp")
    n_dev = lax.axis_size("dev")
    rows_here = samples.shape[0]
    total = rows_here * n_grp * n_dev
    inv_root = jnp.float32(1.0) / jnp.sqrt(jnp.float32(total))

    meta, words = pack_meta(set_labels, sign_words)
    own = jnp.concatenate([samples, meta], axis=1)
    own_wide = jnp.concatenate([own, corpus], axis=1)

    grp_bits = axis_order(n_grp, GRP_ORDER)
    halves = [own[: rows_here // 2], own[rows_here // 2:]]
    col_buf, col_order = xor_gather(own_wide, "grp", n_grp, grp_bits)
    blk_bufs = [xor_gather(h, "dev", n_dev, axis_order(n_dev, o))[0] for h, o in zip(halves, DEV_ORDERS)]

    col_buf = col_buf.reshape(n_grp * rows_here, -1)
    col_rows, col_vec = unpack(col_buf[:, :D + META], words)
    col_corpus = col_buf[:, D + META:]
    col_sq = squares(col_rows)
    corpus_sq = squares(col_corpus)

    forms_part = 0.0
    proof_sum = 0.0
    for blk_buf in blk_bufs:
        blk_buf = blk_buf.reshape(-1, blk_buf.shape[-1])
        block_rows, block_vec = unpack(blk_buf, words)
        block_sq = squares(block_rows)
        dist = distances(block_rows, block_sq, col_rows, col_sq)
        block_wide = block_vec.astype(jnp.float32)
        forms = []
        for kernel_id in range(NB):
            kern = jnp.exp(-dist * scales[kernel_id]).astype(jnp.bfloat16)
            product = jnp.dot(kern, col_vec, preferred_element_type=jnp.float32)
            forms.append(jnp.sum(block_wide * product, axis=0))
        forms_part = forms_part + jnp.stack(forms)

        cdist = distances(col_corpus, corpus_sq, block_rows, block_sq)
        weights = block_vec[:, 0]
        proofs = []
        for kernel_id in range(NB):
            kern = jnp.exp(-cdist * scales[kernel_id]).astype(jnp.bfloat16)
            proofs.append(jnp.dot(kern, weights, preferred_element_type=jnp.float32))
        proof_sum = proof_sum + jnp.stack(proofs)
    proof_part = proof_sum.reshape(NB, n_grp, rows_here)
    inverse = jnp.asarray(np.argsort(np.array(col_order)), jnp.int32)
    place = inverse[jnp.arange(n_grp, dtype=jnp.int32) ^ lax.axis_index("grp")]
    proof_part = jnp.take(proof_part, place, axis=1)
    proof_part = jnp.transpose(proof_part, (1, 0, 2))
    got = lax.all_to_all(proof_part, "grp", 0, 0, tiled=True)
    proof = jnp.sum(got, axis=0) * inv_root

    quad_forms = xor_sum(forms_part, n_grp, n_dev) / total
    bootstrap = quad_forms[:, 1:]
    centre = jnp.mean(bootstrap, axis=1)
    spread = jnp.mean(jnp.square(bootstrap - centre[:, None]), axis=1)
    test_scores = (quad_forms[:, 0] - centre) / jnp.sqrt(spread + 1e-06)
    return (quad_forms, test_scores, proof)


def solution(mesh):
    in_specs = (
        P(("grp", "dev"), None),
        P(("grp", "dev")),
        P(("grp", "dev"), None),
        P(("grp", "dev"), None),
        P(),
        P(),
    )
    out_specs = (P(), P(), P(None, ("grp", "dev")))
    return jax.shard_map(
        per_device, mesh=mesh, in_specs=in_specs, out_specs=out_specs, check_vma=False
    )
```

```python
import numpy as np
import jax
import jax.numpy as jnp
from jax import lax
from jax.sharding import PartitionSpec as P

NB = 4
BOOT = 511
D = 1024
META = 128
CHUNK = 7


word_bits = 21


def make_vectors(set_labels, sign_words):
    weights = (1 - 2 * set_labels).astype(jnp.float32)
    shifts = jnp.arange(word_bits, dtype=jnp.int32)
    bit_flags = jnp.right_shift(sign_words[:, :, None], shifts[None, None, :]) & 1
    bit_flags = bit_flags.reshape(sign_words.shape[0], -1)[:, :BOOT]
    sign_values = (2 * bit_flags - 1).astype(jnp.float32)
    vectors = jnp.concatenate([weights[:, None], sign_values * weights[:, None]], axis=1)
    return vectors.astype(jnp.bfloat16)


def band_scales(scale_grid, scale_pick):
    onehot = (
        scale_pick[:, None] == jnp.arange(scale_grid.shape[0], dtype=jnp.int32)[None, :]
    ).astype(jnp.float32)
    chosen = jnp.sum(onehot * scale_grid[None, :], axis=1)
    return 0.5 / chosen


def squares(matrix):
    wide = matrix.astype(jnp.float32)
    return jnp.sum(wide * wide, axis=1)


def distances(left, left_sq, right, right_sq):
    cross = lax.dot_general(
        left, right, (((1,), (1,)), ((), ())), preferred_element_type=jnp.float32
    )
    return left_sq[:, None] + right_sq[None, :] - 2.0 * cross


def pack_meta(set_labels, sign_words):
    words = sign_words.shape[1]
    chunks = [(sign_words >> (CHUNK * c)) & ((1 << CHUNK) - 1) for c in range(3)]
    meta = jnp.concatenate([set_labels[:, None]] + chunks, axis=1)
    pad = META - meta.shape[1]
    meta = jnp.pad(meta, ((0, 0), (0, pad)))
    return meta.astype(jnp.bfloat16), words


def unpack(buf, words):
    rows = buf[:, :D]
    meta = buf[:, D:D + 1 + 3 * words].astype(jnp.float32).astype(jnp.int32)
    labels = meta[:, 0]
    c = [meta[:, 1 + k * words:1 + (k + 1) * words] for k in range(3)]
    sign_words = c[0] + (c[1] << CHUNK) + (c[2] << (2 * CHUNK))
    return rows, make_vectors(labels, sign_words)


def xor_gather(x, axis, n, bits):
    idx = lax.axis_index(axis)
    buf = x[None]
    for b in bits:
        k = 1 << b
        other = lax.ppermute(buf, axis, [(i, i ^ k) for i in range(n)])
        lo = (idx & k) == 0
        buf = jnp.where(lo, jnp.concatenate([buf, other]), jnp.concatenate([other, buf]))
    order = [sum(((t >> j) & 1) << b for j, b in enumerate(bits)) for t in range(n)]
    return buf, order


GRP_ORDER = (3, 1, 2, 0)
DEV_ORDERS = ((2, 4, 1, 0, 3), (4, 2, 3, 1, 0))
SUM_ORDER = (("grp", 0), ("dev", 0), ("dev", 1), ("dev", 2), ("grp", 1), ("grp", 2), ("dev", 3), ("dev", 4), ("grp", 3))


def axis_order(n, preferred):
    nbits = n.bit_length() - 1
    bits = [b for b in preferred if b < nbits]
    return bits + [b for b in range(nbits) if b not in bits]


def xor_sum(x, rider, n_grp, n_dev):
    sizes = {"grp": n_grp, "dev": n_dev}
    steps = [(a, b) for a, b in SUM_ORDER if (1 << b) < sizes[a]]
    for a in sizes:
        steps += [(a, b) for b in range(sizes[a].bit_length() - 1) if (a, b) not in steps]
    grp_bits = n_grp.bit_length() - 1
    rider = rider.reshape((rider.shape[0],) + (2,) * grp_bits + (rider.shape[-1],))
    axis_bits = list(range(grp_bits - 1, -1, -1))
    grp_idx = lax.axis_index("grp")
    for a, b in steps:
        pairs = [(i, i ^ (1 << b)) for i in range(sizes[a])]
        if a != "grp":
            x = x + lax.ppermute(x, a, pairs)
            continue
        axis = 1 + axis_bits.index(b)
        axis_bits.remove(b)
        mine = (grp_idx >> b) & 1
        keep = lax.dynamic_index_in_dim(rider, mine, axis, keepdims=False)
        send = lax.dynamic_index_in_dim(rider, 1 - mine, axis, keepdims=False)
        got = lax.ppermute(jnp.concatenate([x.ravel(), send.ravel()]), a, pairs)
        x = x + got[: x.size].reshape(x.shape)
        rider = keep + got[x.size:].reshape(keep.shape)
    return x, rider


def per_device(samples, set_labels, sign_words, corpus, scale_grid, scale_pick):
    scales = band_scales(scale_grid, scale_pick)
    n_grp = lax.axis_size("grp")
    n_dev = lax.axis_size("dev")
    rows_here = samples.shape[0]
    total = rows_here * n_grp * n_dev
    inv_root = jnp.float32(1.0) / jnp.sqrt(jnp.float32(total))

    meta, words = pack_meta(set_labels, sign_words)
    own = jnp.concatenate([samples, meta], axis=1)
    own_wide = jnp.concatenate([own, corpus], axis=1)

    grp_bits = axis_order(n_grp, GRP_ORDER)
    halves = [own[: rows_here // 2], own[rows_here // 2:]]
    col_buf, col_order = xor_gather(own_wide, "grp", n_grp, grp_bits)
    blk_buf = jnp.concatenate(
        [xor_gather(h, "dev", n_dev, axis_order(n_dev, o))[0] for h, o in zip(halves, DEV_ORDERS)], axis=1
    )

    col_buf = col_buf.reshape(n_grp * rows_here, -1)
    blk_buf = blk_buf.reshape(n_dev * rows_here, -1)
    col_rows, col_vec = unpack(col_buf[:, :D + META], words)
    col_corpus = col_buf[:, D + META:]
    block_rows, block_vec = unpack(blk_buf, words)

    col_sq = squares(col_rows)
    block_sq = squares(block_rows)

    dist = distances(block_rows, block_sq, col_rows, col_sq)
    block_wide = block_vec.astype(jnp.float32)
    forms = []
    for kernel_id in range(NB):
        kern = jnp.exp(-dist * scales[kernel_id]).astype(jnp.bfloat16)
        product = jnp.dot(kern, col_vec, preferred_element_type=jnp.float32)
        forms.append(jnp.sum(block_wide * product, axis=0))
    forms_part = jnp.stack(forms)

    cdist = distances(col_corpus, squares(col_corpus), block_rows, block_sq)
    weights = block_vec[:, 0]
    proofs = []
    for kernel_id in range(NB):
        kern = jnp.exp(-cdist * scales[kernel_id]).astype(jnp.bfloat16)
        proofs.append(jnp.dot(kern, weights, preferred_element_type=jnp.float32))
    proof_part = jnp.stack(proofs).reshape(NB, n_grp, rows_here)
    inverse = np.argsort(np.array(col_order))
    proof_part = jnp.take(proof_part, jnp.asarray(inverse, jnp.int32), axis=1)
    quad_forms, proof = xor_sum(forms_part, proof_part, n_grp, n_dev)
    quad_forms = quad_forms / total
    proof = proof * inv_root
    bootstrap = quad_forms[:, 1:]
    centre = jnp.mean(bootstrap, axis=1)
    spread = jnp.mean(jnp.square(bootstrap - centre[:, None]), axis=1)
    test_scores = (quad_forms[:, 0] - centre) / jnp.sqrt(spread + 1e-06)
    return (quad_forms, test_scores, proof)


def solution(mesh):
    in_specs = (
        P(("grp", "dev"), None),
        P(("grp", "dev")),
        P(("grp", "dev"), None),
        P(("grp", "dev"), None),
        P(),
        P(),
    )
    out_specs = (P(), P(), P(None, ("grp", "dev")))
    return jax.shard_map(
        per_device, mesh=mesh, in_specs=in_specs, out_specs=out_specs, check_vma=False
    )
```

```python
import numpy as np
import jax
import jax.numpy as jnp
from jax import lax
from jax.sharding import PartitionSpec as P

NB = 4
BOOT = 511
D = 1024
META = 128
CHUNK = 7


word_bits = 21


def make_vectors(set_labels, sign_words):
    weights = (1 - 2 * set_labels).astype(jnp.float32)
    shifts = jnp.arange(word_bits, dtype=jnp.int32)
    bit_flags = jnp.right_shift(sign_words[:, :, None], shifts[None, None, :]) & 1
    bit_flags = bit_flags.reshape(sign_words.shape[0], -1)[:, :BOOT]
    sign_values = (2 * bit_flags - 1).astype(jnp.float32)
    vectors = jnp.concatenate([weights[:, None], sign_values * weights[:, None]], axis=1)
    return vectors.astype(jnp.bfloat16)


def band_scales(scale_grid, scale_pick):
    onehot = (
        scale_pick[:, None] == jnp.arange(scale_grid.shape[0], dtype=jnp.int32)[None, :]
    ).astype(jnp.float32)
    chosen = jnp.sum(onehot * scale_grid[None, :], axis=1)
    return 0.5 / chosen


def squares(matrix):
    wide = matrix.astype(jnp.float32)
    return jnp.sum(wide * wide, axis=1)


def distances(left, left_sq, right, right_sq):
    cross = lax.dot_general(
        left, right, (((1,), (1,)), ((), ())), preferred_element_type=jnp.float32
    )
    return left_sq[:, None] + right_sq[None, :] - 2.0 * cross


def pack_meta(set_labels, sign_words):
    words = sign_words.shape[1]
    chunks = [(sign_words >> (CHUNK * c)) & ((1 << CHUNK) - 1) for c in range(3)]
    meta = jnp.concatenate([set_labels[:, None]] + chunks, axis=1)
    pad = META - meta.shape[1]
    meta = jnp.pad(meta, ((0, 0), (0, pad)))
    return meta.astype(jnp.bfloat16), words


def unpack(buf, words):
    rows = buf[:, :D]
    meta = buf[:, D:D + 1 + 3 * words].astype(jnp.float32).astype(jnp.int32)
    labels = meta[:, 0]
    c = [meta[:, 1 + k * words:1 + (k + 1) * words] for k in range(3)]
    sign_words = c[0] + (c[1] << CHUNK) + (c[2] << (2 * CHUNK))
    return rows, make_vectors(labels, sign_words)


def xor_gather(x, axis, n, bits):
    idx = lax.axis_index(axis)
    buf = x[None]
    for b in bits:
        k = 1 << b
        other = lax.ppermute(buf, axis, [(i, i ^ k) for i in range(n)])
        lo = (idx & k) == 0
        buf = jnp.where(lo, jnp.concatenate([buf, other]), jnp.concatenate([other, buf]))
    order = [sum(((t >> j) & 1) << b for j, b in enumerate(bits)) for t in range(n)]
    return buf, order


GRP_ORDER = (3, 1, 2, 0)
DEV_ORDERS = ((2, 4, 1, 0, 3), (4, 2, 3, 1, 0))
SUM_ORDER = (("grp", 0), ("dev", 0), ("dev", 1), ("dev", 2), ("grp", 1), ("grp", 2), ("dev", 3), ("dev", 4), ("grp", 3))


def axis_order(n, preferred):
    nbits = n.bit_length() - 1
    bits = [b for b in preferred if b < nbits]
    return bits + [b for b in range(nbits) if b not in bits]


def xor_sum(x, rider, n_grp, n_dev):
    sizes = {"grp": n_grp, "dev": n_dev}
    steps = [(a, b) for a, b in SUM_ORDER if (1 << b) < sizes[a]]
    for a in sizes:
        steps += [(a, b) for b in range(sizes[a].bit_length() - 1) if (a, b) not in steps]
    grp_bits = n_grp.bit_length() - 1
    rider = rider.reshape((rider.shape[0],) + (2,) * grp_bits + (rider.shape[-1],))
    axis_bits = list(range(grp_bits - 1, -1, -1))
    grp_idx = lax.axis_index("grp")
    for a, b in steps:
        pairs = [(i, i ^ (1 << b)) for i in range(sizes[a])]
        if a != "grp":
            x = x + lax.ppermute(x, a, pairs)
            continue
        axis = 1 + axis_bits.index(b)
        axis_bits.remove(b)
        mine = (grp_idx >> b) & 1
        keep = lax.dynamic_index_in_dim(rider, mine, axis, keepdims=False)
        send = lax.dynamic_index_in_dim(rider, 1 - mine, axis, keepdims=False)
        got = lax.ppermute(jnp.concatenate([x.ravel(), send.ravel()]), a, pairs)
        x = x + got[: x.size].reshape(x.shape)
        rider = keep + got[x.size:].reshape(keep.shape)
    return x, rider


def per_device(samples, set_labels, sign_words, corpus, scale_grid, scale_pick):
    scales = band_scales(scale_grid, scale_pick)
    n_grp = lax.axis_size("grp")
    n_dev = lax.axis_size("dev")
    rows_here = samples.shape[0]
    total = rows_here * n_grp * n_dev
    inv_root = jnp.float32(1.0) / jnp.sqrt(jnp.float32(total))

    meta, words = pack_meta(set_labels, sign_words)
    own = jnp.concatenate([samples, meta], axis=1)
    own_wide = jnp.concatenate([own, corpus], axis=1)

    grp_bits = axis_order(n_grp, GRP_ORDER)
    halves = [own[: rows_here // 2], own[rows_here // 2:]]
    col_buf = lax.all_to_all(jnp.broadcast_to(own_wide[None], (n_grp,) + own_wide.shape), "grp", 0, 0, tiled=True)
    col_order = list(range(n_grp))
    blk_buf = jnp.concatenate(
        [xor_gather(h, "dev", n_dev, axis_order(n_dev, o))[0] for h, o in zip(halves, DEV_ORDERS)], axis=1
    )

    col_buf = col_buf.reshape(n_grp * rows_here, -1)
    blk_buf = blk_buf.reshape(n_dev * rows_here, -1)
    col_rows, col_vec = unpack(col_buf[:, :D + META], words)
    col_corpus = col_buf[:, D + META:]
    block_rows, block_vec = unpack(blk_buf, words)

    col_sq = squares(col_rows)
    block_sq = squares(block_rows)

    dist = distances(block_rows, block_sq, col_rows, col_sq)
    block_wide = block_vec.astype(jnp.float32)
    forms = []
    for kernel_id in range(NB):
        kern = jnp.exp(-dist * scales[kernel_id]).astype(jnp.bfloat16)
        product = jnp.dot(kern, col_vec, preferred_element_type=jnp.float32)
        forms.append(jnp.sum(block_wide * product, axis=0))
    forms_part = jnp.stack(forms)

    cdist = distances(col_corpus, squares(col_corpus), block_rows, block_sq)
    weights = block_vec[:, 0]
    proofs = []
    for kernel_id in range(NB):
        kern = jnp.exp(-cdist * scales[kernel_id]).astype(jnp.bfloat16)
        proofs.append(jnp.dot(kern, weights, preferred_element_type=jnp.float32))
    proof_part = jnp.stack(proofs).reshape(NB, n_grp, rows_here)
    inverse = np.argsort(np.array(col_order))
    proof_part = jnp.take(proof_part, jnp.asarray(inverse, jnp.int32), axis=1)
    quad_forms, proof = xor_sum(forms_part, proof_part, n_grp, n_dev)
    quad_forms = quad_forms / total
    proof = proof * inv_root
    bootstrap = quad_forms[:, 1:]
    centre = jnp.mean(bootstrap, axis=1)
    spread = jnp.mean(jnp.square(bootstrap - centre[:, None]), axis=1)
    test_scores = (quad_forms[:, 0] - centre) / jnp.sqrt(spread + 1e-06)
    return (quad_forms, test_scores, proof)


def solution(mesh):
    in_specs = (
        P(("grp", "dev"), None),
        P(("grp", "dev")),
        P(("grp", "dev"), None),
        P(("grp", "dev"), None),
        P(),
        P(),
    )
    out_specs = (P(), P(), P(None, ("grp", "dev")))
    return jax.shard_map(
        per_device, mesh=mesh, in_specs=in_specs, out_specs=out_specs, check_vma=False
    )
```

```python
import numpy as np
import jax
import jax.numpy as jnp
from jax import lax
from jax.sharding import PartitionSpec as P

NB = 4
BOOT = 511
D = 1024
META = 128
CHUNK = 7


word_bits = 21


def make_vectors(set_labels, sign_words):
    weights = (1 - 2 * set_labels).astype(jnp.float32)
    shifts = jnp.arange(word_bits, dtype=jnp.int32)
    bit_flags = jnp.right_shift(sign_words[:, :, None], shifts[None, None, :]) & 1
    bit_flags = bit_flags.reshape(sign_words.shape[0], -1)[:, :BOOT]
    sign_values = (2 * bit_flags - 1).astype(jnp.float32)
    vectors = jnp.concatenate([weights[:, None], sign_values * weights[:, None]], axis=1)
    return vectors.astype(jnp.bfloat16)


def band_scales(scale_grid, scale_pick):
    onehot = (
        scale_pick[:, None] == jnp.arange(scale_grid.shape[0], dtype=jnp.int32)[None, :]
    ).astype(jnp.float32)
    chosen = jnp.sum(onehot * scale_grid[None, :], axis=1)
    return 0.5 / chosen


def squares(matrix):
    wide = matrix.astype(jnp.float32)
    return jnp.sum(wide * wide, axis=1)


def distances(left, left_sq, right, right_sq):
    cross = lax.dot_general(
        left, right, (((1,), (1,)), ((), ())), preferred_element_type=jnp.float32
    )
    return left_sq[:, None] + right_sq[None, :] - 2.0 * cross


def pack_meta(set_labels, sign_words):
    words = sign_words.shape[1]
    chunks = [(sign_words >> (CHUNK * c)) & ((1 << CHUNK) - 1) for c in range(3)]
    meta = jnp.concatenate([set_labels[:, None]] + chunks, axis=1)
    pad = META - meta.shape[1]
    meta = jnp.pad(meta, ((0, 0), (0, pad)))
    return meta.astype(jnp.bfloat16), words


def unpack(buf, words):
    rows = buf[:, :D]
    meta = buf[:, D:D + 1 + 3 * words].astype(jnp.float32).astype(jnp.int32)
    labels = meta[:, 0]
    c = [meta[:, 1 + k * words:1 + (k + 1) * words] for k in range(3)]
    sign_words = c[0] + (c[1] << CHUNK) + (c[2] << (2 * CHUNK))
    return rows, make_vectors(labels, sign_words)


def xor_gather(x, axis, n, bits, buf=None):
    idx = lax.axis_index(axis)
    buf = x[None] if buf is None else buf
    for b in bits:
        k = 1 << b
        other = lax.ppermute(buf, axis, [(i, i ^ k) for i in range(n)])
        lo = (idx & k) == 0
        buf = jnp.where(lo, jnp.concatenate([buf, other]), jnp.concatenate([other, buf]))
    order = [sum(((t >> j) & 1) << b for j, b in enumerate(bits)) for t in range(n)]
    return buf, order


GRP_ORDER = (3, 1, 2, 0)
DEV_JOINT = (2, 4)
DEV_ORDERS = ((1, 0, 3), (3, 1, 0))
SUM_ORDER = (("grp", 0), ("dev", 0), ("dev", 1), ("dev", 2), ("grp", 1), ("grp", 2), ("dev", 3), ("dev", 4), ("grp", 3))


def axis_order(n, preferred):
    nbits = n.bit_length() - 1
    bits = [b for b in preferred if b < nbits]
    return bits + [b for b in range(nbits) if b not in bits]


def xor_sum(x, rider, n_grp, n_dev):
    sizes = {"grp": n_grp, "dev": n_dev}
    steps = [(a, b) for a, b in SUM_ORDER if (1 << b) < sizes[a]]
    for a in sizes:
        steps += [(a, b) for b in range(sizes[a].bit_length() - 1) if (a, b) not in steps]
    grp_bits = n_grp.bit_length() - 1
    rider = rider.reshape((rider.shape[0],) + (2,) * grp_bits + (rider.shape[-1],))
    axis_bits = list(range(grp_bits - 1, -1, -1))
    grp_idx = lax.axis_index("grp")
    for a, b in steps:
        pairs = [(i, i ^ (1 << b)) for i in range(sizes[a])]
        if a != "grp":
            x = x + lax.ppermute(x, a, pairs)
            continue
        axis = 1 + axis_bits.index(b)
        axis_bits.remove(b)
        mine = (grp_idx >> b) & 1
        keep = lax.dynamic_index_in_dim(rider, mine, axis, keepdims=False)
        send = lax.dynamic_index_in_dim(rider, 1 - mine, axis, keepdims=False)
        got = lax.ppermute(jnp.concatenate([x.ravel(), send.ravel()]), a, pairs)
        x = x + got[: x.size].reshape(x.shape)
        rider = keep + got[x.size:].reshape(keep.shape)
    return x, rider


def per_device(samples, set_labels, sign_words, corpus, scale_grid, scale_pick):
    scales = band_scales(scale_grid, scale_pick)
    n_grp = lax.axis_size("grp")
    n_dev = lax.axis_size("dev")
    rows_here = samples.shape[0]
    total = rows_here * n_grp * n_dev
    inv_root = jnp.float32(1.0) / jnp.sqrt(jnp.float32(total))

    meta, words = pack_meta(set_labels, sign_words)
    own = jnp.concatenate([samples, meta], axis=1)
    own_wide = jnp.concatenate([own, corpus], axis=1)

    grp_bits = axis_order(n_grp, GRP_ORDER)
    dev_nbits = n_dev.bit_length() - 1
    joint = [b for b in DEV_JOINT if b < dev_nbits]
    col_buf, col_order = xor_gather(own_wide, "grp", n_grp, grp_bits)
    blk_buf, _ = xor_gather(own, "dev", n_dev, joint)
    half = rows_here // 2
    parts = []
    for h, o in zip((blk_buf[:, :half], blk_buf[:, half:]), DEV_ORDERS):
        rest = axis_order(n_dev, [b for b in o if b not in joint])
        rest = [b for b in rest if b not in joint]
        parts.append(xor_gather(None, "dev", n_dev, rest, buf=h)[0])
    blk_buf = jnp.concatenate(parts, axis=1)

    col_buf = col_buf.reshape(n_grp * rows_here, -1)
    blk_buf = blk_buf.reshape(n_dev * rows_here, -1)
    col_rows, col_vec = unpack(col_buf[:, :D + META], words)
    col_corpus = col_buf[:, D + META:]
    block_rows, block_vec = unpack(blk_buf, words)

    col_sq = squares(col_rows)
    block_sq = squares(block_rows)

    dist = distances(block_rows, block_sq, col_rows, col_sq)
    block_wide = block_vec.astype(jnp.float32)
    forms = []
    for kernel_id in range(NB):
        kern = jnp.exp(-dist * scales[kernel_id]).astype(jnp.bfloat16)
        product = jnp.dot(kern, col_vec, preferred_element_type=jnp.float32)
        forms.append(jnp.sum(block_wide * product, axis=0))
    forms_part = jnp.stack(forms)

    cdist = distances(col_corpus, squares(col_corpus), block_rows, block_sq)
    weights = block_vec[:, 0]
    proofs = []
    for kernel_id in range(NB):
        kern = jnp.exp(-cdist * scales[kernel_id]).astype(jnp.bfloat16)
        proofs.append(jnp.dot(kern, weights, preferred_element_type=jnp.float32))
    proof_part = jnp.stack(proofs).reshape(NB, n_grp, rows_here)
    inverse = np.argsort(np.array(col_order))
    proof_part = jnp.take(proof_part, jnp.asarray(inverse, jnp.int32), axis=1)
    quad_forms, proof = xor_sum(forms_part, proof_part, n_grp, n_dev)
    quad_forms = quad_forms / total
    proof = proof * inv_root
    bootstrap = quad_forms[:, 1:]
    centre = jnp.mean(bootstrap, axis=1)
    spread = jnp.mean(jnp.square(bootstrap - centre[:, None]), axis=1)
    test_scores = (quad_forms[:, 0] - centre) / jnp.sqrt(spread + 1e-06)
    return (quad_forms, test_scores, proof)


def solution(mesh):
    in_specs = (
        P(("grp", "dev"), None),
        P(("grp", "dev")),
        P(("grp", "dev"), None),
        P(("grp", "dev"), None),
        P(),
        P(),
    )
    out_specs = (P(), P(), P(None, ("grp", "dev")))
    return jax.shard_map(
        per_device, mesh=mesh, in_specs=in_specs, out_specs=out_specs, check_vma=False
    )
```

```python
import numpy as np
import jax
import jax.numpy as jnp
from jax import lax
from jax.sharding import PartitionSpec as P

NB = 4
BOOT = 511
D = 1024
META = 128
CHUNK = 7


word_bits = 21


def make_vectors(set_labels, sign_words):
    weights = (1 - 2 * set_labels).astype(jnp.float32)
    shifts = jnp.arange(word_bits, dtype=jnp.int32)
    bit_flags = jnp.right_shift(sign_words[:, :, None], shifts[None, None, :]) & 1
    bit_flags = bit_flags.reshape(sign_words.shape[0], -1)[:, :BOOT]
    sign_values = (2 * bit_flags - 1).astype(jnp.float32)
    vectors = jnp.concatenate([weights[:, None], sign_values * weights[:, None]], axis=1)
    return vectors.astype(jnp.bfloat16)


def band_scales(scale_grid, scale_pick):
    onehot = (
        scale_pick[:, None] == jnp.arange(scale_grid.shape[0], dtype=jnp.int32)[None, :]
    ).astype(jnp.float32)
    chosen = jnp.sum(onehot * scale_grid[None, :], axis=1)
    return 0.5 / chosen


def squares(matrix):
    wide = matrix.astype(jnp.float32)
    return jnp.sum(wide * wide, axis=1)


def distances(left, left_sq, right, right_sq):
    cross = lax.dot_general(
        left, right, (((1,), (1,)), ((), ())), preferred_element_type=jnp.float32
    )
    return left_sq[:, None] + right_sq[None, :] - 2.0 * cross


def split3(x):
    hi = lax.reduce_precision(x, exponent_bits=8, mantissa_bits=7)
    rest = x - hi
    mid = lax.reduce_precision(rest, exponent_bits=8, mantissa_bits=7)
    lo = rest - mid
    return jnp.stack([hi, mid, lo], axis=1).astype(jnp.bfloat16)


def join3(parts):
    wide = parts.astype(jnp.float32)
    return (wide[:, 0] + wide[:, 1]) + wide[:, 2]


def pack_meta(set_labels, sign_words, samples, corpus):
    words = sign_words.shape[1]
    chunks = [(sign_words >> (CHUNK * c)) & ((1 << CHUNK) - 1) for c in range(3)]
    meta = jnp.concatenate([set_labels[:, None]] + chunks, axis=1).astype(jnp.bfloat16)
    meta = jnp.concatenate([meta, split3(squares(samples)), split3(squares(corpus))], axis=1)
    pad = META - meta.shape[1]
    meta = jnp.pad(meta, ((0, 0), (0, pad)))
    return meta, words


def unpack(buf, words):
    rows = buf[:, :D]
    meta = buf[:, D:D + 1 + 3 * words].astype(jnp.float32).astype(jnp.int32)
    labels = meta[:, 0]
    c = [meta[:, 1 + k * words:1 + (k + 1) * words] for k in range(3)]
    sign_words = c[0] + (c[1] << CHUNK) + (c[2] << (2 * CHUNK))
    at = D + 1 + 3 * words
    return rows, make_vectors(labels, sign_words), join3(buf[:, at:at + 3]), join3(buf[:, at + 3:at + 6])


def xor_gather(x, axis, n, bits, buf=None):
    idx = lax.axis_index(axis)
    buf = x[None] if buf is None else buf
    for b in bits:
        k = 1 << b
        other = lax.ppermute(buf, axis, [(i, i ^ k) for i in range(n)])
        lo = (idx & k) == 0
        buf = jnp.where(lo, jnp.concatenate([buf, other]), jnp.concatenate([other, buf]))
    order = [sum(((t >> j) & 1) << b for j, b in enumerate(bits)) for t in range(n)]
    return buf, order


GRP_ORDER = (3, 1, 2, 0)
DEV_JOINT = (2, 4)
DEV_ORDERS = ((1, 0, 3), (3, 1, 0))
SUM_ORDER = (("dev", 0), ("dev", 1), ("dev", 2), ("dev", 3), ("dev", 4), ("grp", 0), ("grp", 1), ("grp", 2), ("grp", 3))


def axis_order(n, preferred):
    nbits = n.bit_length() - 1
    bits = [b for b in preferred if b < nbits]
    return bits + [b for b in range(nbits) if b not in bits]


def xor_sum(x, rider, n_grp, n_dev):
    sizes = {"grp": n_grp, "dev": n_dev}
    steps = [(a, b) for a, b in SUM_ORDER if (1 << b) < sizes[a]]
    for a in sizes:
        steps += [(a, b) for b in range(sizes[a].bit_length() - 1) if (a, b) not in steps]
    grp_bits = n_grp.bit_length() - 1
    rider = rider.reshape((rider.shape[0],) + (2,) * grp_bits + (rider.shape[-1],))
    axis_bits = list(range(grp_bits - 1, -1, -1))
    grp_idx = lax.axis_index("grp")
    for a, b in steps:
        pairs = [(i, i ^ (1 << b)) for i in range(sizes[a])]
        if a != "grp":
            x = x + lax.ppermute(x, a, pairs)
            continue
        axis = 1 + axis_bits.index(b)
        axis_bits.remove(b)
        mine = (grp_idx >> b) & 1
        keep = lax.dynamic_index_in_dim(rider, mine, axis, keepdims=False)
        send = lax.dynamic_index_in_dim(rider, 1 - mine, axis, keepdims=False)
        got = lax.ppermute(jnp.concatenate([x.ravel(), send.ravel()]), a, pairs)
        x = x + got[: x.size].reshape(x.shape)
        rider = keep + got[x.size:].reshape(keep.shape)
    return x, rider


def per_device(samples, set_labels, sign_words, corpus, scale_grid, scale_pick):
    scales = band_scales(scale_grid, scale_pick)
    n_grp = lax.axis_size("grp")
    n_dev = lax.axis_size("dev")
    rows_here = samples.shape[0]
    total = rows_here * n_grp * n_dev
    inv_root = jnp.float32(1.0) / jnp.sqrt(jnp.float32(total))

    meta, words = pack_meta(set_labels, sign_words, samples, corpus)
    own = jnp.concatenate([samples, meta], axis=1)
    own_wide = jnp.concatenate([own, corpus], axis=1)

    grp_bits = axis_order(n_grp, GRP_ORDER)
    dev_nbits = n_dev.bit_length() - 1
    joint = [b for b in DEV_JOINT if b < dev_nbits]
    col_buf, col_order = xor_gather(own_wide, "grp", n_grp, grp_bits)
    blk_buf, _ = xor_gather(own, "dev", n_dev, joint)
    half = rows_here // 2
    parts = []
    for h, o in zip((blk_buf[:, :half], blk_buf[:, half:]), DEV_ORDERS):
        rest = axis_order(n_dev, [b for b in o if b not in joint])
        rest = [b for b in rest if b not in joint]
        parts.append(xor_gather(None, "dev", n_dev, rest, buf=h)[0])
    blk_buf = jnp.concatenate(parts, axis=1)

    col_buf = col_buf.reshape(n_grp * rows_here, -1)
    blk_buf = blk_buf.reshape(n_dev * rows_here, -1)
    col_rows, col_vec, col_sq, corpus_sq = unpack(col_buf[:, :D + META], words)
    col_corpus = col_buf[:, D + META:]
    block_rows, block_vec, block_sq, _ = unpack(blk_buf, words)


    dist = distances(block_rows, block_sq, col_rows, col_sq)
    block_wide = block_vec.astype(jnp.float32)
    forms = []
    for kernel_id in range(NB):
        kern = jnp.exp(-dist * scales[kernel_id]).astype(jnp.bfloat16)
        product = jnp.dot(kern, col_vec, preferred_element_type=jnp.float32)
        forms.append(jnp.sum(block_wide * product, axis=0))
    forms_part = jnp.stack(forms)

    cdist = distances(col_corpus, corpus_sq, block_rows, block_sq)
    weights = block_vec[:, 0]
    proofs = []
    for kernel_id in range(NB):
        kern = jnp.exp(-cdist * scales[kernel_id]).astype(jnp.bfloat16)
        proofs.append(jnp.dot(kern, weights, preferred_element_type=jnp.float32))
    proof_part = jnp.stack(proofs).reshape(NB, n_grp, rows_here)
    inverse = np.argsort(np.array(col_order))
    proof_part = jnp.take(proof_part, jnp.asarray(inverse, jnp.int32), axis=1)
    quad_forms, proof = xor_sum(forms_part, proof_part, n_grp, n_dev)
    quad_forms = quad_forms / total
    proof = proof * inv_root
    bootstrap = quad_forms[:, 1:]
    centre = jnp.mean(bootstrap, axis=1)
    spread = jnp.mean(jnp.square(bootstrap - centre[:, None]), axis=1)
    test_scores = (quad_forms[:, 0] - centre) / jnp.sqrt(spread + 1e-06)
    return (quad_forms, test_scores, proof)


def solution(mesh):
    in_specs = (
        P(("grp", "dev"), None),
        P(("grp", "dev")),
        P(("grp", "dev"), None),
        P(("grp", "dev"), None),
        P(),
        P(),
    )
    out_specs = (P(), P(), P(None, ("grp", "dev")))
    return jax.shard_map(
        per_device, mesh=mesh, in_specs=in_specs, out_specs=out_specs, check_vma=False
    )
```

```python
import numpy as np
import jax
import jax.numpy as jnp
from jax import lax
from jax.sharding import PartitionSpec as P

NB = 4
BOOT = 511
D = 1024
META = 128
CHUNK = 7


word_bits = 21


def make_vectors(set_labels, sign_words):
    weights = (1 - 2 * set_labels).astype(jnp.float32)
    shifts = jnp.arange(word_bits, dtype=jnp.int32)
    bit_flags = jnp.right_shift(sign_words[:, :, None], shifts[None, None, :]) & 1
    bit_flags = bit_flags.reshape(sign_words.shape[0], -1)[:, :BOOT]
    sign_values = (2 * bit_flags - 1).astype(jnp.float32)
    vectors = jnp.concatenate([weights[:, None], sign_values * weights[:, None]], axis=1)
    return vectors.astype(jnp.bfloat16)


def band_scales(scale_grid, scale_pick):
    onehot = (
        scale_pick[:, None] == jnp.arange(scale_grid.shape[0], dtype=jnp.int32)[None, :]
    ).astype(jnp.float32)
    chosen = jnp.sum(onehot * scale_grid[None, :], axis=1)
    return 0.5 / chosen


def squares(matrix):
    wide = matrix.astype(jnp.float32)
    return jnp.sum(wide * wide, axis=1)


def distances(left, left_sq, right, right_sq):
    cross = lax.dot_general(
        left, right, (((1,), (1,)), ((), ())), preferred_element_type=jnp.float32
    )
    return left_sq[:, None] + right_sq[None, :] - 2.0 * cross


def split3(x):
    hi = lax.reduce_precision(x, exponent_bits=8, mantissa_bits=7)
    rest = x - hi
    mid = lax.reduce_precision(rest, exponent_bits=8, mantissa_bits=7)
    lo = rest - mid
    return jnp.stack([hi, mid, lo], axis=1).astype(jnp.bfloat16)


def join3(parts):
    wide = parts.astype(jnp.float32)
    return (wide[:, 0] + wide[:, 1]) + wide[:, 2]


def pack_meta(set_labels, sign_words, samples, corpus):
    words = sign_words.shape[1]
    chunks = [(sign_words >> (CHUNK * c)) & ((1 << CHUNK) - 1) for c in range(3)]
    meta = jnp.concatenate([set_labels[:, None]] + chunks, axis=1).astype(jnp.bfloat16)
    norms = jnp.concatenate([split3(squares(samples)), split3(squares(corpus))], axis=1)
    pad = META - meta.shape[1]
    plain = jnp.pad(meta, ((0, 0), (0, pad)))
    with_norms = jnp.pad(jnp.concatenate([meta, norms], axis=1), ((0, 0), (0, pad - norms.shape[1])))
    return plain, with_norms, words


def unpack(buf, words):
    rows = buf[:, :D]
    meta = buf[:, D:D + 1 + 3 * words].astype(jnp.float32).astype(jnp.int32)
    labels = meta[:, 0]
    c = [meta[:, 1 + k * words:1 + (k + 1) * words] for k in range(3)]
    sign_words = c[0] + (c[1] << CHUNK) + (c[2] << (2 * CHUNK))
    at = D + 1 + 3 * words
    return rows, make_vectors(labels, sign_words), join3(buf[:, at:at + 3]), join3(buf[:, at + 3:at + 6])


def xor_gather(x, axis, n, bits, buf=None):
    idx = lax.axis_index(axis)
    buf = x[None] if buf is None else buf
    for b in bits:
        k = 1 << b
        other = lax.ppermute(buf, axis, [(i, i ^ k) for i in range(n)])
        lo = (idx & k) == 0
        buf = jnp.where(lo, jnp.concatenate([buf, other]), jnp.concatenate([other, buf]))
    order = [sum(((t >> j) & 1) << b for j, b in enumerate(bits)) for t in range(n)]
    return buf, order


GRP_ORDER = (3, 1, 2, 0)
DEV_JOINT = (2, 4)
DEV_ORDERS = ((1, 0, 3), (3, 1, 0))
SUM_ORDER = (("dev", 0), ("dev", 1), ("dev", 2), ("dev", 3), ("dev", 4), ("grp", 0), ("grp", 1), ("grp", 2), ("grp", 3))


def axis_order(n, preferred):
    nbits = n.bit_length() - 1
    bits = [b for b in preferred if b < nbits]
    return bits + [b for b in range(nbits) if b not in bits]


def xor_sum(x, rider, n_grp, n_dev):
    sizes = {"grp": n_grp, "dev": n_dev}
    steps = [(a, b) for a, b in SUM_ORDER if (1 << b) < sizes[a]]
    for a in sizes:
        steps += [(a, b) for b in range(sizes[a].bit_length() - 1) if (a, b) not in steps]
    grp_bits = n_grp.bit_length() - 1
    rider = rider.reshape((rider.shape[0],) + (2,) * grp_bits + (rider.shape[-1],))
    axis_bits = list(range(grp_bits - 1, -1, -1))
    grp_idx = lax.axis_index("grp")
    for a, b in steps:
        pairs = [(i, i ^ (1 << b)) for i in range(sizes[a])]
        if a != "grp":
            x = x + lax.ppermute(x, a, pairs)
            continue
        axis = 1 + axis_bits.index(b)
        axis_bits.remove(b)
        mine = (grp_idx >> b) & 1
        keep = lax.dynamic_index_in_dim(rider, mine, axis, keepdims=False)
        send = lax.dynamic_index_in_dim(rider, 1 - mine, axis, keepdims=False)
        got = lax.ppermute(jnp.concatenate([x.ravel(), send.ravel()]), a, pairs)
        x = x + got[: x.size].reshape(x.shape)
        rider = keep + got[x.size:].reshape(keep.shape)
    return x, rider


def body(samples, set_labels, sign_words, corpus, scale_grid, scale_pick):
    scales = band_scales(scale_grid, scale_pick)
    n_grp = lax.axis_size("grp")
    n_dev = lax.axis_size("dev")
    rows_here = samples.shape[0]
    total = rows_here * n_grp * n_dev
    inv_root = jnp.float32(1.0) / jnp.sqrt(jnp.float32(total))

    meta, meta_norms, words = pack_meta(set_labels, sign_words, samples, corpus)
    own = jnp.concatenate([samples, meta], axis=1)
    own_wide = jnp.concatenate([samples, meta_norms, corpus], axis=1)

    grp_bits = axis_order(n_grp, GRP_ORDER)
    dev_nbits = n_dev.bit_length() - 1
    joint = [b for b in DEV_JOINT if b < dev_nbits]
    col_buf, col_order = xor_gather(own_wide, "grp", n_grp, grp_bits)
    blk_buf, _ = xor_gather(own, "dev", n_dev, joint)
    half = rows_here // 2
    parts = []
    for h, o in zip((blk_buf[:, :half], blk_buf[:, half:]), DEV_ORDERS):
        rest = axis_order(n_dev, [b for b in o if b not in joint])
        rest = [b for b in rest if b not in joint]
        parts.append(xor_gather(None, "dev", n_dev, rest, buf=h)[0])
    blk_buf = jnp.concatenate(parts, axis=1)

    col_buf = col_buf.reshape(n_grp * rows_here, -1)
    blk_buf = blk_buf.reshape(n_dev * rows_here, -1)
    col_rows, col_vec, col_sq, corpus_sq = unpack(col_buf[:, :D + META], words)
    col_corpus = col_buf[:, D + META:]
    block_rows, block_vec, _, _ = unpack(blk_buf, words)
    block_sq = squares(block_rows)


    dist = distances(block_rows, block_sq, col_rows, col_sq)
    block_wide = block_vec.astype(jnp.float32)
    forms = []
    for kernel_id in range(NB):
        kern = jnp.exp(-dist * scales[kernel_id]).astype(jnp.bfloat16)
        product = jnp.dot(kern, col_vec, preferred_element_type=jnp.float32)
        forms.append(jnp.sum(block_wide * product, axis=0))
    forms_part = jnp.stack(forms)

    cdist = distances(col_corpus, corpus_sq, block_rows, block_sq)
    weights = block_vec[:, 0]
    proofs = []
    for kernel_id in range(NB):
        kern = jnp.exp(-cdist * scales[kernel_id]).astype(jnp.bfloat16)
        proofs.append(jnp.dot(kern, weights, preferred_element_type=jnp.float32))
    proof_part = jnp.stack(proofs).reshape(NB, n_grp, rows_here)
    inverse = np.argsort(np.array(col_order))
    proof_part = jnp.take(proof_part, jnp.asarray(inverse, jnp.int32), axis=1)
    quad_forms, proof = xor_sum(forms_part, proof_part, n_grp, n_dev)
    quad_forms = quad_forms / total
    proof = proof * inv_root
    bootstrap = quad_forms[:, 1:]
    centre = jnp.mean(bootstrap, axis=1)
    spread = jnp.mean(jnp.square(bootstrap - centre[:, None]), axis=1)
    test_scores = (quad_forms[:, 0] - centre) / jnp.sqrt(spread + 1e-06)
    return (quad_forms, test_scores, proof)


def solution(mesh):
    in_specs = (
        P(("grp", "dev"), None),
        P(("grp", "dev")),
        P(("grp", "dev"), None),
        P(("grp", "dev"), None),
        P(),
        P(),
    )
    out_specs = (P(), P(), P(None, ("grp", "dev")))
    return jax.shard_map(body, mesh=mesh, in_specs=in_specs, out_specs=out_specs, check_vma=False)
```

```python
import numpy as np
import jax
import jax.numpy as jnp
from jax import lax
from jax.sharding import PartitionSpec as P

NB = 4
BOOT = 511
D = 1024
META = 128
CHUNK = 7


word_bits = 21


def make_vectors(set_labels, sign_words):
    weights = (1 - 2 * set_labels).astype(jnp.float32)
    shifts = jnp.arange(word_bits, dtype=jnp.int32)
    bit_flags = jnp.right_shift(sign_words[:, :, None], shifts[None, None, :]) & 1
    bit_flags = bit_flags.reshape(sign_words.shape[0], -1)[:, :BOOT]
    sign_values = (2 * bit_flags - 1).astype(jnp.float32)
    vectors = jnp.concatenate([weights[:, None], sign_values * weights[:, None]], axis=1)
    return vectors.astype(jnp.bfloat16)


def band_scales(scale_grid, scale_pick):
    onehot = (
        scale_pick[:, None] == jnp.arange(scale_grid.shape[0], dtype=jnp.int32)[None, :]
    ).astype(jnp.float32)
    chosen = jnp.sum(onehot * scale_grid[None, :], axis=1)
    return 0.5 / chosen


def squares(matrix):
    wide = matrix.astype(jnp.float32)
    return jnp.sum(wide * wide, axis=1)


def distances(left, left_sq, right, right_sq):
    cross = lax.dot_general(
        left, right, (((1,), (1,)), ((), ())), preferred_element_type=jnp.float32
    )
    return left_sq[:, None] + right_sq[None, :] - 2.0 * cross


def split3(x):
    hi = lax.reduce_precision(x, exponent_bits=8, mantissa_bits=7)
    rest = x - hi
    mid = lax.reduce_precision(rest, exponent_bits=8, mantissa_bits=7)
    lo = rest - mid
    return jnp.stack([hi, mid, lo], axis=1).astype(jnp.bfloat16)


def join3(parts):
    wide = parts.astype(jnp.float32)
    return (wide[:, 0] + wide[:, 1]) + wide[:, 2]


def pack_meta(set_labels, sign_words, samples, corpus):
    words = sign_words.shape[1]
    chunks = [(sign_words >> (CHUNK * c)) & ((1 << CHUNK) - 1) for c in range(3)]
    meta = jnp.concatenate([set_labels[:, None]] + chunks, axis=1).astype(jnp.bfloat16)
    norms = jnp.concatenate([split3(squares(samples)), split3(squares(corpus))], axis=1)
    pad = META - meta.shape[1]
    plain = jnp.pad(meta, ((0, 0), (0, pad)))
    with_norms = jnp.pad(jnp.concatenate([meta, norms], axis=1), ((0, 0), (0, pad - norms.shape[1])))
    return plain, with_norms, words


def unpack(buf, words):
    rows = buf[:, :D]
    meta = buf[:, D:D + 1 + 3 * words].astype(jnp.float32).astype(jnp.int32)
    labels = meta[:, 0]
    c = [meta[:, 1 + k * words:1 + (k + 1) * words] for k in range(3)]
    sign_words = c[0] + (c[1] << CHUNK) + (c[2] << (2 * CHUNK))
    at = D + 1 + 3 * words
    return rows, make_vectors(labels, sign_words), join3(buf[:, at:at + 3]), join3(buf[:, at + 3:at + 6])


def xor_gather(x, axis, n, bits, buf=None):
    idx = lax.axis_index(axis)
    buf = x[None] if buf is None else buf
    for b in bits:
        k = 1 << b
        other = lax.ppermute(buf, axis, [(i, i ^ k) for i in range(n)])
        lo = (idx & k) == 0
        buf = jnp.where(lo, jnp.concatenate([buf, other]), jnp.concatenate([other, buf]))
    order = [sum(((t >> j) & 1) << b for j, b in enumerate(bits)) for t in range(n)]
    return buf, order


GRP_ORDER = (3, 1, 2, 0)
DEV_JOINT = (2, 4)
DEV_ORDERS = ((1, 0, 3), (3, 1, 0))
SUM_ORDER = (("dev", 0), ("dev", 1), ("dev", 2), ("dev", 3), ("dev", 4), ("grp", 0), ("grp", 1), ("grp", 2), ("grp", 3))


def axis_order(n, preferred):
    nbits = n.bit_length() - 1
    bits = [b for b in preferred if b < nbits]
    return bits + [b for b in range(nbits) if b not in bits]


def xor_sum(x, rider, n_grp, n_dev):
    sizes = {"grp": n_grp, "dev": n_dev}
    steps = [(a, b) for a, b in SUM_ORDER if (1 << b) < sizes[a]]
    for a in sizes:
        steps += [(a, b) for b in range(sizes[a].bit_length() - 1) if (a, b) not in steps]
    grp_bits = n_grp.bit_length() - 1
    rider = rider.reshape((rider.shape[0],) + (2,) * grp_bits + (rider.shape[-1],))
    axis_bits = list(range(grp_bits - 1, -1, -1))
    grp_idx = lax.axis_index("grp")
    for a, b in steps:
        pairs = [(i, i ^ (1 << b)) for i in range(sizes[a])]
        if a != "grp":
            x = x + lax.ppermute(x, a, pairs)
            continue
        axis = 1 + axis_bits.index(b)
        axis_bits.remove(b)
        mine = (grp_idx >> b) & 1
        keep = lax.dynamic_index_in_dim(rider, mine, axis, keepdims=False)
        send = lax.dynamic_index_in_dim(rider, 1 - mine, axis, keepdims=False)
        got = lax.ppermute(jnp.concatenate([x.ravel(), send.ravel()]), a, pairs)
        x = x + got[: x.size].reshape(x.shape)
        rider = keep + got[x.size:].reshape(keep.shape)
    return x, rider


def body(samples, set_labels, sign_words, corpus, scale_grid, scale_pick):
    scales = band_scales(scale_grid, scale_pick)
    n_grp = lax.axis_size("grp")
    n_dev = lax.axis_size("dev")
    rows_here = samples.shape[0]
    total = rows_here * n_grp * n_dev
    inv_root = jnp.float32(1.0) / jnp.sqrt(jnp.float32(total))

    _, meta_norms, words = pack_meta(set_labels, sign_words, samples, corpus)
    own = jnp.concatenate([samples, meta_norms], axis=1)
    own_wide = jnp.concatenate([own, corpus], axis=1)

    grp_bits = axis_order(n_grp, GRP_ORDER)
    dev_nbits = n_dev.bit_length() - 1
    joint = [b for b in DEV_JOINT if b < dev_nbits]
    col_buf, col_order = xor_gather(own_wide, "grp", n_grp, grp_bits)
    blk_buf, _ = xor_gather(own, "dev", n_dev, joint)
    half = rows_here // 2
    parts = []
    for h, o in zip((blk_buf[:, :half], blk_buf[:, half:]), DEV_ORDERS):
        rest = axis_order(n_dev, [b for b in o if b not in joint])
        rest = [b for b in rest if b not in joint]
        parts.append(xor_gather(None, "dev", n_dev, rest, buf=h)[0])
    blk_buf = jnp.concatenate(parts, axis=1)

    col_buf = col_buf.reshape(n_grp * rows_here, -1)
    blk_buf = blk_buf.reshape(n_dev * rows_here, -1)
    col_rows, col_vec, col_sq, corpus_sq = unpack(col_buf[:, :D + META], words)
    col_corpus = col_buf[:, D + META:]
    block_rows, block_vec, block_sq, _ = unpack(blk_buf, words)


    dist = distances(block_rows, block_sq, col_rows, col_sq)
    block_wide = block_vec.astype(jnp.float32)
    forms = []
    for kernel_id in range(NB):
        kern = jnp.exp(-dist * scales[kernel_id]).astype(jnp.bfloat16)
        product = jnp.dot(kern, col_vec, preferred_element_type=jnp.float32)
        forms.append(jnp.sum(block_wide * product, axis=0))
    forms_part = jnp.stack(forms)

    cdist = distances(col_corpus, corpus_sq, block_rows, block_sq)
    weights = block_vec[:, 0]
    proofs = []
    for kernel_id in range(NB):
        kern = jnp.exp(-cdist * scales[kernel_id]).astype(jnp.bfloat16)
        proofs.append(jnp.dot(kern, weights, preferred_element_type=jnp.float32))
    proof_part = jnp.stack(proofs).reshape(NB, n_grp, rows_here)
    inverse = np.argsort(np.array(col_order))
    proof_part = jnp.take(proof_part, jnp.asarray(inverse, jnp.int32), axis=1)
    quad_forms, proof = xor_sum(forms_part, proof_part, n_grp, n_dev)
    quad_forms = quad_forms / total
    proof = proof * inv_root
    bootstrap = quad_forms[:, 1:]
    centre = jnp.mean(bootstrap, axis=1)
    spread = jnp.mean(jnp.square(bootstrap - centre[:, None]), axis=1)
    test_scores = (quad_forms[:, 0] - centre) / jnp.sqrt(spread + 1e-06)
    return (quad_forms, test_scores, proof)


def solution(mesh):
    in_specs = (
        P(("grp", "dev"), None),
        P(("grp", "dev")),
        P(("grp", "dev"), None),
        P(("grp", "dev"), None),
        P(),
        P(),
    )
    out_specs = (P(), P(), P(None, ("grp", "dev")))
    return jax.shard_map(body, mesh=mesh, in_specs=in_specs, out_specs=out_specs, check_vma=False)
```

```python
import numpy as np
import jax
import jax.numpy as jnp
from jax import lax
from jax.sharding import PartitionSpec as P

NB = 4
BOOT = 511
D = 1024
META = 128
CHUNK = 7


word_bits = 21


def make_vectors(set_labels, sign_words):
    weights = (1 - 2 * set_labels).astype(jnp.float32)
    shifts = jnp.arange(word_bits, dtype=jnp.int32)
    bit_flags = jnp.right_shift(sign_words[:, :, None], shifts[None, None, :]) & 1
    bit_flags = bit_flags.reshape(sign_words.shape[0], -1)[:, :BOOT]
    sign_values = (2 * bit_flags - 1).astype(jnp.float32)
    vectors = jnp.concatenate([weights[:, None], sign_values * weights[:, None]], axis=1)
    return vectors.astype(jnp.bfloat16)


def band_scales(scale_grid, scale_pick):
    onehot = (
        scale_pick[:, None] == jnp.arange(scale_grid.shape[0], dtype=jnp.int32)[None, :]
    ).astype(jnp.float32)
    chosen = jnp.sum(onehot * scale_grid[None, :], axis=1)
    return 0.5 / chosen


def squares(matrix):
    wide = matrix.astype(jnp.float32)
    return jnp.sum(wide * wide, axis=1)


def distances(left, left_sq, right, right_sq):
    cross = lax.dot_general(
        left, right, (((1,), (1,)), ((), ())), preferred_element_type=jnp.float32
    )
    return left_sq[:, None] + right_sq[None, :] - 2.0 * cross


def split3(x):
    hi = lax.reduce_precision(x, exponent_bits=8, mantissa_bits=7)
    rest = x - hi
    mid = lax.reduce_precision(rest, exponent_bits=8, mantissa_bits=7)
    lo = rest - mid
    return jnp.stack([hi, mid, lo], axis=1).astype(jnp.bfloat16)


def join3(parts):
    wide = parts.astype(jnp.float32)
    return (wide[:, 0] + wide[:, 1]) + wide[:, 2]


def pack_meta(set_labels, sign_words, samples, corpus):
    words = sign_words.shape[1]
    chunks = [(sign_words >> (CHUNK * c)) & ((1 << CHUNK) - 1) for c in range(3)]
    meta = jnp.concatenate([set_labels[:, None]] + chunks, axis=1).astype(jnp.bfloat16)
    norms = jnp.concatenate([split3(squares(samples)), split3(squares(corpus))], axis=1)
    pad = META - meta.shape[1]
    plain = jnp.pad(meta, ((0, 0), (0, pad)))
    with_norms = jnp.pad(jnp.concatenate([meta, norms], axis=1), ((0, 0), (0, pad - norms.shape[1])))
    return plain, with_norms, words


def unpack(buf, words):
    rows = buf[:, :D]
    meta = buf[:, D:D + 1 + 3 * words].astype(jnp.float32).astype(jnp.int32)
    labels = meta[:, 0]
    c = [meta[:, 1 + k * words:1 + (k + 1) * words] for k in range(3)]
    sign_words = c[0] + (c[1] << CHUNK) + (c[2] << (2 * CHUNK))
    at = D + 1 + 3 * words
    return rows, make_vectors(labels, sign_words), join3(buf[:, at:at + 3]), join3(buf[:, at + 3:at + 6])


def xor_gather(x, axis, n, bits, buf=None):
    idx = lax.axis_index(axis)
    buf = x[None] if buf is None else buf
    for b in bits:
        k = 1 << b
        other = lax.ppermute(buf, axis, [(i, i ^ k) for i in range(n)])
        lo = (idx & k) == 0
        buf = jnp.where(lo, jnp.concatenate([buf, other]), jnp.concatenate([other, buf]))
    order = [sum(((t >> j) & 1) << b for j, b in enumerate(bits)) for t in range(n)]
    return buf, order


GRP_ORDER = (3, 1, 2, 0)
DEV_JOINT = (2, 4)
DEV_ORDERS = ((1, 0, 3), (3, 1, 0))
SUM_ORDER = (("dev", 0), ("dev", 1), ("dev", 2), ("dev", 3), ("dev", 4), ("grp", 0), ("grp", 1), ("grp", 2), ("grp", 3))


def axis_order(n, preferred):
    nbits = n.bit_length() - 1
    bits = [b for b in preferred if b < nbits]
    return bits + [b for b in range(nbits) if b not in bits]


def xor_sum(x, rider, n_grp, n_dev):
    sizes = {"grp": n_grp, "dev": n_dev}
    steps = [(a, b) for a, b in SUM_ORDER if (1 << b) < sizes[a]]
    for a in sizes:
        steps += [(a, b) for b in range(sizes[a].bit_length() - 1) if (a, b) not in steps]
    grp_bits = n_grp.bit_length() - 1
    rider = rider.reshape((rider.shape[0],) + (2,) * grp_bits + (rider.shape[-1],))
    axis_bits = list(range(grp_bits - 1, -1, -1))
    grp_idx = lax.axis_index("grp")
    for a, b in steps:
        pairs = [(i, i ^ (1 << b)) for i in range(sizes[a])]
        if a != "grp":
            x = x + lax.ppermute(x, a, pairs)
            continue
        axis = 1 + axis_bits.index(b)
        axis_bits.remove(b)
        mine = (grp_idx >> b) & 1
        keep = lax.dynamic_index_in_dim(rider, mine, axis, keepdims=False)
        send = lax.dynamic_index_in_dim(rider, 1 - mine, axis, keepdims=False)
        got = lax.ppermute(jnp.concatenate([x.ravel(), send.ravel()]), a, pairs)
        x = x + got[: x.size].reshape(x.shape)
        rider = keep + got[x.size:].reshape(keep.shape)
    return x, rider


def proof_terms(col_corpus, corpus_sq, block_rows, block_sq, block_vec, scales):
    cdist = distances(col_corpus, corpus_sq, block_rows, block_sq)
    weights = block_vec[:, 0]
    proofs = []
    for kernel_id in range(NB):
        kern = jnp.exp(-cdist * scales[kernel_id]).astype(jnp.bfloat16)
        proofs.append(jnp.dot(kern, weights, preferred_element_type=jnp.float32))
    return jnp.stack(proofs)


def body(samples, set_labels, sign_words, corpus, scale_grid, scale_pick):
    scales = band_scales(scale_grid, scale_pick)
    n_grp = lax.axis_size("grp")
    n_dev = lax.axis_size("dev")
    rows_here = samples.shape[0]
    total = rows_here * n_grp * n_dev
    inv_root = jnp.float32(1.0) / jnp.sqrt(jnp.float32(total))

    _, meta_norms, words = pack_meta(set_labels, sign_words, samples, corpus)
    own = jnp.concatenate([samples, meta_norms], axis=1)
    own_wide = jnp.concatenate([own, corpus], axis=1)

    grp_bits = axis_order(n_grp, GRP_ORDER)
    dev_nbits = n_dev.bit_length() - 1
    joint = [b for b in DEV_JOINT if b < dev_nbits]
    col_buf, col_order = xor_gather(own_wide, "grp", n_grp, grp_bits)
    blk_buf, _ = xor_gather(own, "dev", n_dev, joint)
    half = rows_here // 2
    parts = []
    for h, o in zip((blk_buf[:, :half], blk_buf[:, half:]), DEV_ORDERS):
        rest = axis_order(n_dev, [b for b in o if b not in joint])
        rest = [b for b in rest if b not in joint]
        parts.append(xor_gather(None, "dev", n_dev, rest, buf=h)[0])
    blk_buf = jnp.concatenate(parts, axis=1)

    col_buf = col_buf.reshape(n_grp * rows_here, -1)
    blk_buf = blk_buf.reshape(n_dev * rows_here, -1)
    col_rows, col_vec, col_sq, corpus_sq = unpack(col_buf[:, :D + META], words)
    col_corpus = col_buf[:, D + META:]
    block_rows, block_vec, block_sq, _ = unpack(blk_buf, words)


    dist = distances(block_rows, block_sq, col_rows, col_sq)
    block_wide = block_vec.astype(jnp.float32)
    forms = []
    for kernel_id in range(NB):
        kern = jnp.exp(-dist * scales[kernel_id]).astype(jnp.bfloat16)
        product = jnp.dot(kern, col_vec, preferred_element_type=jnp.float32)
        forms.append(jnp.sum(block_wide * product, axis=0))
    forms_part = jnp.stack(forms)

    proof_part = proof_terms(col_corpus, corpus_sq, block_rows, block_sq, block_vec, scales)
    proof_part = proof_part.reshape(NB, n_grp, rows_here)
    inverse = np.argsort(np.array(col_order))
    proof_part = jnp.take(proof_part, jnp.asarray(inverse, jnp.int32), axis=1)
    quad_forms, proof = xor_sum(forms_part, proof_part, n_grp, n_dev)
    quad_forms = quad_forms / total
    proof = proof * inv_root
    bootstrap = quad_forms[:, 1:]
    centre = jnp.mean(bootstrap, axis=1)
    spread = jnp.mean(jnp.square(bootstrap - centre[:, None]), axis=1)
    test_scores = (quad_forms[:, 0] - centre) / jnp.sqrt(spread + 1e-06)
    return (quad_forms, test_scores, proof)


def solution(mesh):
    in_specs = (
        P(("grp", "dev"), None),
        P(("grp", "dev")),
        P(("grp", "dev"), None),
        P(("grp", "dev"), None),
        P(),
        P(),
    )
    out_specs = (P(), P(), P(None, ("grp", "dev")))
    return jax.shard_map(body, mesh=mesh, in_specs=in_specs, out_specs=out_specs, check_vma=False)
```

```python
import numpy as np
import jax
import jax.numpy as jnp
from jax import lax
from jax.sharding import PartitionSpec as P

NB = 4
BOOT = 511
D = 1024
META = 128
CHUNK = 7


word_bits = 21


def make_vectors(set_labels, sign_words):
    weights = (1 - 2 * set_labels).astype(jnp.float32)
    shifts = jnp.arange(word_bits, dtype=jnp.int32)
    bit_flags = jnp.right_shift(sign_words[:, :, None], shifts[None, None, :]) & 1
    bit_flags = bit_flags.reshape(sign_words.shape[0], -1)[:, :BOOT]
    sign_values = (2 * bit_flags - 1).astype(jnp.float32)
    vectors = jnp.concatenate([weights[:, None], sign_values * weights[:, None]], axis=1)
    return vectors.astype(jnp.bfloat16)


def band_scales(scale_grid, scale_pick):
    onehot = (
        scale_pick[:, None] == jnp.arange(scale_grid.shape[0], dtype=jnp.int32)[None, :]
    ).astype(jnp.float32)
    chosen = jnp.sum(onehot * scale_grid[None, :], axis=1)
    return 0.5 / chosen


def squares(matrix):
    wide = matrix.astype(jnp.float32)
    return jnp.sum(wide * wide, axis=1)


def distances(left, left_sq, right, right_sq):
    cross = lax.dot_general(
        left, right, (((1,), (1,)), ((), ())), preferred_element_type=jnp.float32
    )
    return left_sq[:, None] + right_sq[None, :] - 2.0 * cross


def split3(x):
    hi = lax.reduce_precision(x, exponent_bits=8, mantissa_bits=7)
    rest = x - hi
    mid = lax.reduce_precision(rest, exponent_bits=8, mantissa_bits=7)
    lo = rest - mid
    return jnp.stack([hi, mid, lo], axis=1).astype(jnp.bfloat16)


def join3(parts):
    wide = parts.astype(jnp.float32)
    return (wide[:, 0] + wide[:, 1]) + wide[:, 2]


def pack_meta(set_labels, sign_words, samples, corpus):
    words = sign_words.shape[1]
    chunks = [(sign_words >> (CHUNK * c)) & ((1 << CHUNK) - 1) for c in range(3)]
    meta = jnp.concatenate([set_labels[:, None]] + chunks, axis=1).astype(jnp.bfloat16)
    norms = jnp.concatenate([split3(squares(samples)), split3(squares(corpus))], axis=1)
    pad = META - meta.shape[1]
    plain = jnp.pad(meta, ((0, 0), (0, pad)))
    with_norms = jnp.pad(jnp.concatenate([meta, norms], axis=1), ((0, 0), (0, pad - norms.shape[1])))
    return plain, with_norms, words


def unpack(buf, words):
    rows = buf[:, :D]
    meta = buf[:, D:D + 1 + 3 * words].astype(jnp.float32).astype(jnp.int32)
    labels = meta[:, 0]
    c = [meta[:, 1 + k * words:1 + (k + 1) * words] for k in range(3)]
    sign_words = c[0] + (c[1] << CHUNK) + (c[2] << (2 * CHUNK))
    at = D + 1 + 3 * words
    return rows, make_vectors(labels, sign_words), join3(buf[:, at:at + 3]), join3(buf[:, at + 3:at + 6])


def xor_gather(x, axis, n, bits, buf=None, ordered=True):
    idx = lax.axis_index(axis)
    buf = x[None] if buf is None else buf
    for b in bits:
        k = 1 << b
        other = lax.ppermute(buf, axis, [(i, i ^ k) for i in range(n)])
        if not ordered:
            buf = jnp.concatenate([buf, other])
            continue
        lo = (idx & k) == 0
        buf = jnp.where(lo, jnp.concatenate([buf, other]), jnp.concatenate([other, buf]))
    order = [sum(((t >> j) & 1) << b for j, b in enumerate(bits)) for t in range(n)]
    return buf, order


GRP_ORDER = (3, 1, 2, 0)
DEV_JOINT = (2, 4)
DEV_ORDERS = ((1, 0, 3), (3, 1, 0))
SUM_ORDER = (("dev", 0), ("dev", 1), ("dev", 2), ("dev", 3), ("dev", 4), ("grp", 0), ("grp", 1), ("grp", 2), ("grp", 3))


def axis_order(n, preferred):
    nbits = n.bit_length() - 1
    bits = [b for b in preferred if b < nbits]
    return bits + [b for b in range(nbits) if b not in bits]


def xor_sum(x, rider, n_grp, n_dev):
    sizes = {"grp": n_grp, "dev": n_dev}
    steps = [(a, b) for a, b in SUM_ORDER if (1 << b) < sizes[a]]
    for a in sizes:
        steps += [(a, b) for b in range(sizes[a].bit_length() - 1) if (a, b) not in steps]
    grp_bits = n_grp.bit_length() - 1
    rider = rider.reshape((rider.shape[0],) + (2,) * grp_bits + (rider.shape[-1],))
    axis_bits = list(range(grp_bits - 1, -1, -1))
    grp_idx = lax.axis_index("grp")
    for a, b in steps:
        pairs = [(i, i ^ (1 << b)) for i in range(sizes[a])]
        if a != "grp":
            x = x + lax.ppermute(x, a, pairs)
            continue
        axis = 1 + axis_bits.index(b)
        axis_bits.remove(b)
        mine = (grp_idx >> b) & 1
        keep = lax.dynamic_index_in_dim(rider, mine, axis, keepdims=False)
        send = lax.dynamic_index_in_dim(rider, 1 - mine, axis, keepdims=False)
        got = lax.ppermute(jnp.concatenate([x.ravel(), send.ravel()]), a, pairs)
        x = x + got[: x.size].reshape(x.shape)
        rider = keep + got[x.size:].reshape(keep.shape)
    return x, rider


def body(samples, set_labels, sign_words, corpus, scale_grid, scale_pick):
    scales = band_scales(scale_grid, scale_pick)
    n_grp = lax.axis_size("grp")
    n_dev = lax.axis_size("dev")
    rows_here = samples.shape[0]
    total = rows_here * n_grp * n_dev
    inv_root = jnp.float32(1.0) / jnp.sqrt(jnp.float32(total))

    _, meta_norms, words = pack_meta(set_labels, sign_words, samples, corpus)
    own = jnp.concatenate([samples, meta_norms], axis=1)
    own_wide = jnp.concatenate([own, corpus], axis=1)

    grp_bits = axis_order(n_grp, GRP_ORDER)
    dev_nbits = n_dev.bit_length() - 1
    joint = [b for b in DEV_JOINT if b < dev_nbits]
    col_buf, col_order = xor_gather(own_wide, "grp", n_grp, grp_bits)
    blk_buf, _ = xor_gather(own, "dev", n_dev, joint, ordered=False)
    half = rows_here // 2
    parts = []
    for h, o in zip((blk_buf[:, :half], blk_buf[:, half:]), DEV_ORDERS):
        rest = axis_order(n_dev, [b for b in o if b not in joint])
        rest = [b for b in rest if b not in joint]
        parts.append(xor_gather(None, "dev", n_dev, rest, buf=h, ordered=False)[0])
    blk_buf = jnp.concatenate(parts, axis=1)

    col_buf = col_buf.reshape(n_grp * rows_here, -1)
    blk_buf = blk_buf.reshape(n_dev * rows_here, -1)
    col_rows, col_vec, col_sq, corpus_sq = unpack(col_buf[:, :D + META], words)
    col_corpus = col_buf[:, D + META:]
    block_rows, block_vec, block_sq, _ = unpack(blk_buf, words)


    dist = distances(block_rows, block_sq, col_rows, col_sq)
    block_wide = block_vec.astype(jnp.float32)
    forms = []
    for kernel_id in range(NB):
        kern = jnp.exp(-dist * scales[kernel_id]).astype(jnp.bfloat16)
        product = jnp.dot(kern, col_vec, preferred_element_type=jnp.float32)
        forms.append(jnp.sum(block_wide * product, axis=0))
    forms_part = jnp.stack(forms)

    cdist = distances(col_corpus, corpus_sq, block_rows, block_sq)
    weights = block_vec[:, 0]
    proofs = []
    for kernel_id in range(NB):
        kern = jnp.exp(-cdist * scales[kernel_id]).astype(jnp.bfloat16)
        proofs.append(jnp.dot(kern, weights, preferred_element_type=jnp.float32))
    proof_part = jnp.stack(proofs).reshape(NB, n_grp, rows_here)
    inverse = np.argsort(np.array(col_order))
    proof_part = jnp.take(proof_part, jnp.asarray(inverse, jnp.int32), axis=1)
    quad_forms, proof = xor_sum(forms_part, proof_part, n_grp, n_dev)
    quad_forms = quad_forms / total
    proof = proof * inv_root
    bootstrap = quad_forms[:, 1:]
    centre = jnp.mean(bootstrap, axis=1)
    spread = jnp.mean(jnp.square(bootstrap - centre[:, None]), axis=1)
    test_scores = (quad_forms[:, 0] - centre) / jnp.sqrt(spread + 1e-06)
    return (quad_forms, test_scores, proof)


def solution(mesh):
    in_specs = (
        P(("grp", "dev"), None),
        P(("grp", "dev")),
        P(("grp", "dev"), None),
        P(("grp", "dev"), None),
        P(),
        P(),
    )
    out_specs = (P(), P(), P(None, ("grp", "dev")))
    return jax.shard_map(body, mesh=mesh, in_specs=in_specs, out_specs=out_specs, check_vma=False)
```
